128 devices in a mesh: row: 8 (over y, core), col: 16 (over z, x).
Axes of the slice: x: 4, y: 4, z: 4, core: 2. Of those that a mesh axis runs over, the one named last changes fastest.
Arguments:
- forward_head: bfloat16 [4, 2048, 1000], P(None, 'col'), may hold values from -6 to 6
- forward_tail: bfloat16 [57344, 1000], P(('col', 'row')), may hold values from -6 to 6
- forward_inverse: bfloat16 [4, 2048, 2048], P(None, 'col', 'row'), may hold values from -1.5 to 1.5, as said below
- forward_coupling: bfloat16 [6, 2048, 2048], P(None, 'row', 'col'), may hold values from -0.078125 to 0.078125
- forward_slab: bfloat16 [4, 2048, 57344], P(None, 'row', 'col'), may hold values from -0.0625 to 0.0625
- backward_head: bfloat16 [4, 2048, 1000], P(None, 'row'), may hold values from -6 to 6
- backward_tail: bfloat16 [57344, 1000], P(('row', 'col')), may hold values from -6 to 6
- backward_inverse: bfloat16 [4, 2048, 2048], P(None, 'col', 'row'), may hold values from -1.5 to 1.5, as said below
- backward_coupling: bfloat16 [6, 2048, 2048], P(None, 'row', 'col'), may hold values from -0.078125 to 0.078125
- backward_slab: bfloat16 [57344, 4, 2048], P('row', None, 'col'), may hold values from -0.0625 to 0.0625
Outputs:
- lower_head: bfloat16 [4, 2048, 1000], P(None, 'row')
- lower_tail: bfloat16 [57344, 1000], P(('col', 'row'))
- upper_head: bfloat16 [4, 2048, 1000], P(None, 'col')
- upper_tail: bfloat16 [57344, 1000], P(('row', 'col'))
The draws below stay inside these ranges and needn't reach their ends.
Inputs may be any that keep to these rules, and one draw needn't show every extreme that they name: Each block of forward_inverse is upper triangular with diagonal entries of magnitude 0.5 to 1.5. Each block of backward_inverse is upper triangular with diagonal entries of magnitude 0.5 to 1.5.
All inputs are finite; a program needn't handle non-finite values.
Results may differ from the reference program's by a relative error of at most 0.03.
Values may be sent and summed in bfloat16 or wider, within the bound.
No kernel may reach another device: no remote copies, remote signals or barrier semaphores. Data moves between devices by JAX's collectives and lax.ppermute only.
A program may use at most 192 MiB of HBM per device.

```python
import jax
import jax.numpy as jnp
from jax import lax

K = 1000
PANEL = 2048
NP = 4
NTAIL = 57344
N_ROW = 8
N_COL = 16


def upper_inverse(key):
    key_spread, key_size, key_sign = jax.random.split(key, 3)
    spread = jnp.clip(jax.random.normal(key_spread, (NP, PANEL, PANEL), jnp.float32), -4.0, 4.0)
    positions = jnp.arange(PANEL)
    upper = (positions[:, None] < positions[None, :]).astype(jnp.float32)
    identity = (positions[:, None] == positions[None, :]).astype(jnp.float32)
    magnitude = jax.random.uniform(key_size, (NP, PANEL), jnp.float32, 0.5, 1.5)
    signs = jnp.where(jax.random.bernoulli(key_sign, 0.5, (NP, PANEL)), 1.0, -1.0)
    diagonal = identity[None, :, :] * (magnitude * signs)[:, None, :]
    result = spread * upper[None, :, :] / jnp.sqrt(jnp.float32(PANEL)) + diagonal
    return result.astype(jnp.bfloat16)


def draw_forward_inverse(key, part):
    return upper_inverse(jax.random.fold_in(key, 11))


def draw_backward_inverse(key, part):
    return upper_inverse(jax.random.fold_in(key, 23))


def level_of(key, extent, pieces, least, largest):
    def one(dim, shards_of):
        steps = jax.random.uniform(jax.random.fold_in(jax.random.fold_in(key, 6), dim), (shards_of,), jnp.float32, least / len(pieces), largest / len(pieces))
        return jnp.repeat(jnp.exp(steps), extent[dim] // shards_of).reshape((-1,) + (1,) * (len(extent) - dim - 1))

    gain = one(*pieces[0])
    for cut in pieces[1:]:
        gain = gain * one(*cut)
    return gain


def normal_values(key, shape, scale, reach, pieces=(), held_as=jnp.bfloat16):
    drawn = jax.random.normal(key, shape, jnp.float32) * scale
    if len(pieces) > 0:
        drawn = level_of(key, shape, pieces, -0.22, 0.18) * drawn
    return jnp.clip(drawn, min=-reach, max=reach).astype(held_as)


def setup_inputs(seed: int = 0) -> dict:
    key_of = jax.random.split(jax.random.key(seed), 11)
    return {
        "forward_head": normal_values(key_of[0], (NP, PANEL, K), 1.0, 6.0, ((1, 16),)),
        "forward_tail": normal_values(key_of[1], (NTAIL, K), 1.0, 6.0, ((0, 128),)),
        "forward_inverse": draw_forward_inverse(jax.random.fold_in(key_of[10], 71), 0),
        "forward_coupling": normal_values(key_of[3], (NP * (NP - 1) // 2, PANEL, PANEL), ((NP - 1) * PANEL) ** -0.5, 0.078125, ((1, 8), (2, 16))),
        "forward_slab": normal_values(key_of[4], (NP, PANEL, NTAIL), (NP * PANEL) ** -0.5, 0.0625, ((1, 8), (2, 16))),
        "backward_head": normal_values(key_of[5], (NP, PANEL, K), 1.0, 6.0, ((1, 8),)),
        "backward_tail": normal_values(key_of[6], (NTAIL, K), 1.0, 6.0, ((0, 128),)),
        "backward_inverse": draw_backward_inverse(jax.random.fold_in(key_of[10], 71), 0),
        "backward_coupling": normal_values(key_of[8], (NP * (NP - 1) // 2, PANEL, PANEL), ((NP - 1) * PANEL) ** -0.5, 0.078125, ((1, 8), (2, 16))),
        "backward_slab": normal_values(key_of[9], (NTAIL, NP, PANEL), (NP * PANEL) ** -0.5, 0.0625, ((0, 8), (2, 16))),
    }


def round_trip(value):
    return lax.optimization_barrier(value.astype(jnp.bfloat16)).astype(jnp.float32)


def reference(forward_head, forward_tail, forward_inverse, forward_coupling, forward_slab, backward_head, backward_tail, backward_inverse, backward_coupling, backward_slab):
    lower_list = []
    for panel_index in range(NP):
        if panel_index == 0:
            adjusted = forward_head[0]
        else:
            summed = jnp.zeros((PANEL, K), jnp.float32)
            for earlier in range(panel_index):
                block = forward_coupling[panel_index * (panel_index - 1) // 2 + earlier]
                summed = summed + jnp.dot(block.T, lower_list[earlier], preferred_element_type=jnp.float32)
            adjusted = (forward_head[panel_index].astype(jnp.float32) - summed).astype(jnp.bfloat16)
        lower_list.append(jnp.dot(forward_inverse[panel_index].T, adjusted, preferred_element_type=jnp.float32).astype(jnp.bfloat16))
    lower_head = jnp.stack(lower_list)
    panel_rows = PANEL // N_ROW
    accumulated = jnp.zeros((NTAIL, K), jnp.float32)
    for group in range(N_ROW):
        slab_piece = forward_slab[:, group * panel_rows:(group + 1) * panel_rows, :].reshape(NP * panel_rows, NTAIL)
        panel_piece = lower_head[:, group * panel_rows:(group + 1) * panel_rows, :].reshape(NP * panel_rows, K)
        partial_value = jnp.dot(slab_piece.T, panel_piece, preferred_element_type=jnp.float32)
        accumulated = accumulated + round_trip(partial_value)
    lower_tail = (forward_tail.astype(jnp.float32) - accumulated).astype(jnp.bfloat16)

    upper_list = [None] * NP
    for panel_index in reversed(range(NP)):
        if panel_index == NP - 1:
            shifted = backward_head[panel_index]
        else:
            summed = jnp.zeros((PANEL, K), jnp.float32)
            for later_panel in range(panel_index + 1, NP):
                block = backward_coupling[later_panel * (later_panel - 1) // 2 + panel_index]
                summed = summed + jnp.dot(block, upper_list[later_panel], preferred_element_type=jnp.float32)
            shifted = (backward_head[panel_index].astype(jnp.float32) - summed).astype(jnp.bfloat16)
        upper_list[panel_index] = jnp.dot(backward_inverse[panel_index], shifted, preferred_element_type=jnp.float32).astype(jnp.bfloat16)
    upper_head = jnp.stack(upper_list)
    panel_cols = PANEL // N_COL
    gathered_sum = jnp.zeros((NTAIL, K), jnp.float32)
    for group in range(N_COL):
        slab_piece = backward_slab[:, :, group * panel_cols:(group + 1) * panel_cols].reshape(NTAIL, NP * panel_cols)
        panel_piece = upper_head[:, group * panel_cols:(group + 1) * panel_cols, :].reshape(NP * panel_cols, K)
        partial_value = jnp.dot(slab_piece, panel_piece, preferred_element_type=jnp.float32)
        gathered_sum = gathered_sum + round_trip(partial_value)
    upper_tail = (backward_tail.astype(jnp.float32) - gathered_sum).astype(jnp.bfloat16)
    return (lower_head, lower_tail, upper_head, upper_tail)
```

```python
import jax
import jax.numpy as jnp
from jax import lax
from jax.sharding import PartitionSpec as P

ROW_INNER = 2
COL_INNER = 4


def shift_pairs(n, inner, sub, d):
    outer = n // inner
    pairs = []
    for o in range(outer):
        for i in range(inner):
            if sub == "inner":
                pairs.append((o * inner + i, o * inner + (i + d) % inner))
            else:
                pairs.append((o * inner + i, ((o + d) % outer) * inner + i))
    return pairs


def sub_index(axis, inner, sub):
    a = lax.axis_index(axis)
    return a % inner if sub == "inner" else a // inner


def sub_size(n, inner, sub):
    return inner if sub == "inner" else n // inner


def ar_direct(v, axis, n, inner, sub):
    size = sub_size(n, inner, sub)
    acc = v.astype(jnp.float32)
    send = v.astype(jnp.bfloat16)
    for d in range(1, size):
        acc = acc + lax.ppermute(send, axis, shift_pairs(n, inner, sub, d)).astype(jnp.float32)
    return acc


def rs_direct(v, axis, n, inner, sub):
    size = sub_size(n, inner, sub)
    me = sub_index(axis, inner, sub)
    pieces = v.reshape(size, v.shape[0] // size, v.shape[1])
    acc = lax.dynamic_index_in_dim(pieces, me, 0, keepdims=False).astype(jnp.float32)
    for d in range(1, size):
        sel = lax.dynamic_index_in_dim(pieces, (me + d) % size, 0, keepdims=False)
        acc = acc + lax.ppermute(
            sel.astype(jnp.bfloat16), axis, shift_pairs(n, inner, sub, d)
        ).astype(jnp.float32)
    return acc


def ag_direct(p, axis, n, inner, sub):
    size = sub_size(n, inner, sub)
    me = sub_index(axis, inner, sub)
    got = [p] + [lax.ppermute(p, axis, shift_pairs(n, inner, sub, -d)) for d in range(1, size)]
    stacked = jnp.roll(jnp.stack(got), me, axis=0)
    return stacked.reshape(size * p.shape[0], p.shape[1])


def allreduce(value, axis, inner):
    n = lax.axis_size(axis)
    piece = rs_direct(value.astype(jnp.bfloat16), axis, n, inner, "inner")
    piece = ar_direct(piece.astype(jnp.bfloat16), axis, n, inner, "outer").astype(jnp.bfloat16)
    return ag_direct(piece, axis, n, inner, "inner")


def reduce_row(value):
    return allreduce(value, "row", ROW_INNER)


def reduce_col(value):
    return allreduce(value, "col", COL_INNER)


def leading_dot(left, right):
    return lax.dot_general(
        left, right, (((0,), (0,)), ((), ())), preferred_element_type=jnp.float32
    )


def local(
    forward_head,
    forward_tail,
    forward_inverse,
    forward_coupling,
    forward_slab,
    backward_head,
    backward_tail,
    backward_inverse,
    backward_coupling,
    backward_slab,
):
    classes = forward_head.shape[2]
    panels = forward_head.shape[0]
    lower_list = []
    for panel_index in range(panels):
        if panel_index == 0:
            adjusted = forward_head[0]
        else:
            summed = leading_dot(
                forward_coupling[panel_index * (panel_index - 1) // 2], lower_list[0]
            )
            for earlier in range(1, panel_index):
                summed = summed + leading_dot(
                    forward_coupling[panel_index * (panel_index - 1) // 2 + earlier],
                    lower_list[earlier],
                )
            coupling = reduce_row(summed).astype(jnp.float32)
            adjusted = (forward_head[panel_index].astype(jnp.float32) - coupling).astype(
                jnp.bfloat16
            )
        lower_list.append(reduce_col(leading_dot(forward_inverse[panel_index], adjusted)))
    lower_head = jnp.stack(lower_list)
    panel_rows = lower_head.shape[1]
    flat_lower = lower_head.reshape(panels * panel_rows, classes)
    flat_slab = forward_slab.reshape(panels * panel_rows, forward_slab.shape[2])
    lower_update = lax.psum_scatter(
        leading_dot(flat_slab, flat_lower).astype(jnp.bfloat16),
        "row",
        scatter_dimension=0,
        tiled=True,
    ).astype(jnp.float32)
    lower_tail = (forward_tail.astype(jnp.float32) - lower_update).astype(jnp.bfloat16)
    upper_list = [None] * panels
    for panel_index in reversed(range(panels)):
        if panel_index == panels - 1:
            shifted = backward_head[panel_index]
        else:
            summed = None
            for later_panel in range(panel_index + 1, panels):
                block = backward_coupling[later_panel * (later_panel - 1) // 2 + panel_index]
                product = jnp.dot(
                    block, upper_list[later_panel], preferred_element_type=jnp.float32
                )
                summed = product if summed is None else summed + product
            pulled = reduce_col(summed).astype(jnp.float32)
            shifted = (backward_head[panel_index].astype(jnp.float32) - pulled).astype(jnp.bfloat16)
        upper_list[panel_index] = reduce_row(
            jnp.dot(backward_inverse[panel_index], shifted, preferred_element_type=jnp.float32)
        )
    upper_head = jnp.stack(upper_list)
    panel_cols = upper_head.shape[1]
    flat_back = backward_slab.reshape(backward_slab.shape[0], panels * panel_cols)
    flat_upper = upper_head.reshape(panels * panel_cols, classes)
    upper_update = lax.psum_scatter(
        jnp.dot(flat_back, flat_upper, preferred_element_type=jnp.float32).astype(jnp.bfloat16),
        "col",
        scatter_dimension=0,
        tiled=True,
    ).astype(jnp.float32)
    upper_tail = (backward_tail.astype(jnp.float32) - upper_update).astype(jnp.bfloat16)
    return (lower_head, lower_tail, upper_head, upper_tail)


def solution(mesh):
    in_specs = (
        P(None, "col", None),
        P(("col", "row"), None),
        P(None, "col", "row"),
        P(None, "row", "col"),
        P(None, "row", "col"),
        P(None, "row", None),
        P(("row", "col"), None),
        P(None, "col", "row"),
        P(None, "row", "col"),
        P("row", None, "col"),
    )
    out_specs = (
        P(None, "row", None),
        P(("col", "row"), None),
        P(None, "col", None),
        P(("row", "col"), None),
    )
    return jax.shard_map(local, mesh=mesh, in_specs=in_specs, out_specs=out_specs, check_vma=False)
```

```python
import jax
import jax.numpy as jnp
from jax import lax
from jax.experimental.layout import Layout, with_layout_constraint
from jax.sharding import PartitionSpec as P

ROW_INNER = 2
COL_INNER = 4


def shift_pairs(n, inner, sub, d):
    outer = n // inner
    pairs = []
    for o in range(outer):
        for i in range(inner):
            if sub == "inner":
                pairs.append((o * inner + i, o * inner + (i + d) % inner))
            else:
                pairs.append((o * inner + i, ((o + d) % outer) * inner + i))
    return pairs


def sub_index(axis, inner, sub):
    a = lax.axis_index(axis)
    return a % inner if sub == "inner" else a // inner


def sub_size(n, inner, sub):
    return inner if sub == "inner" else n // inner


def ar_direct(v, axis, n, inner, sub):
    size = sub_size(n, inner, sub)
    acc = v.astype(jnp.float32)
    send = v.astype(jnp.bfloat16)
    for d in range(1, size):
        acc = acc + lax.ppermute(send, axis, shift_pairs(n, inner, sub, d)).astype(jnp.float32)
    return acc


def rs_direct(v, axis, n, inner, sub):
    size = sub_size(n, inner, sub)
    me = sub_index(axis, inner, sub)
    pieces = v.reshape(size, v.shape[0] // size, v.shape[1])
    acc = lax.dynamic_index_in_dim(pieces, me, 0, keepdims=False).astype(jnp.float32)
    for d in range(1, size):
        sel = lax.dynamic_index_in_dim(pieces, (me + d) % size, 0, keepdims=False)
        acc = acc + lax.ppermute(
            sel.astype(jnp.bfloat16), axis, shift_pairs(n, inner, sub, d)
        ).astype(jnp.float32)
    return acc


def ag_direct(p, axis, n, inner, sub):
    size = sub_size(n, inner, sub)
    me = sub_index(axis, inner, sub)
    got = [p] + [lax.ppermute(p, axis, shift_pairs(n, inner, sub, -d)) for d in range(1, size)]
    stacked = jnp.roll(jnp.stack(got), me, axis=0)
    return stacked.reshape(size * p.shape[0], p.shape[1])


def rs_hier(value, axis, inner):
    n = lax.axis_size(axis)
    outer = n // inner
    rows = value.shape[0] // n
    me_in = sub_index(axis, inner, "inner")
    me_out = sub_index(axis, inner, "outer")
    grid = value.reshape(outer, inner, rows, value.shape[1])
    acc = lax.dynamic_index_in_dim(grid, me_in, 1, keepdims=False).astype(jnp.float32)
    for d in range(1, inner):
        sel = lax.dynamic_index_in_dim(grid, (me_in + d) % inner, 1, keepdims=False)
        acc = acc + lax.ppermute(sel, axis, shift_pairs(n, inner, "inner", d)).astype(jnp.float32)
    half = acc.astype(jnp.bfloat16)
    total = lax.dynamic_index_in_dim(acc, me_out, 0, keepdims=False)
    for d in range(1, outer):
        sel = lax.dynamic_index_in_dim(half, (me_out + d) % outer, 0, keepdims=False)
        total = total + lax.ppermute(sel, axis, shift_pairs(n, inner, "outer", d)).astype(jnp.float32)
    return total


def allreduce(value, axis, inner):
    n = lax.axis_size(axis)
    piece = rs_direct(value.astype(jnp.bfloat16), axis, n, inner, "inner")
    piece = ar_direct(piece.astype(jnp.bfloat16), axis, n, inner, "outer").astype(jnp.bfloat16)
    return ag_direct(piece, axis, n, inner, "inner")


def reduce_row(value):
    return allreduce(value, "row", ROW_INNER)


def reduce_col(value):
    return allreduce(value, "col", COL_INNER)


def leading_dot(left, right):
    return lax.dot_general(
        left, right, (((0,), (0,)), ((), ())), preferred_element_type=jnp.float32
    )


def local(
    forward_head,
    forward_tail,
    forward_inverse,
    forward_coupling,
    forward_slab,
    backward_head,
    backward_tail,
    backward_inverse,
    backward_coupling,
    backward_slab,
):
    classes = forward_head.shape[2]
    panels = forward_head.shape[0]
    lower_list = []
    for panel_index in range(panels):
        if panel_index == 0:
            adjusted = forward_head[0]
        else:
            summed = leading_dot(
                forward_coupling[panel_index * (panel_index - 1) // 2], lower_list[0]
            )
            for earlier in range(1, panel_index):
                summed = summed + leading_dot(
                    forward_coupling[panel_index * (panel_index - 1) // 2 + earlier],
                    lower_list[earlier],
                )
            coupling = reduce_row(summed).astype(jnp.float32)
            adjusted = (forward_head[panel_index].astype(jnp.float32) - coupling).astype(
                jnp.bfloat16
            )
        lower_list.append(reduce_col(leading_dot(forward_inverse[panel_index], adjusted)))
    lower_head = jnp.stack(lower_list)
    panel_rows = lower_head.shape[1]
    flat_lower = lower_head.reshape(panels * panel_rows, classes)
    flat_slab = forward_slab.reshape(panels * panel_rows, forward_slab.shape[2])
    lower_partial = with_layout_constraint(
        leading_dot(flat_slab, flat_lower).astype(jnp.bfloat16), Layout(major_to_minor=(0, 1))
    )
    lower_update = rs_hier(lower_partial, "row", ROW_INNER)
    lower_tail = (forward_tail.astype(jnp.float32) - lower_update).astype(jnp.bfloat16)
    upper_list = [None] * panels
    for panel_index in reversed(range(panels)):
        if panel_index == panels - 1:
            shifted = backward_head[panel_index]
        else:
            summed = None
            for later_panel in range(panel_index + 1, panels):
                block = backward_coupling[later_panel * (later_panel - 1) // 2 + panel_index]
                product = jnp.dot(
                    block, upper_list[later_panel], preferred_element_type=jnp.float32
                )
                summed = product if summed is None else summed + product
            pulled = reduce_col(summed).astype(jnp.float32)
            shifted = (backward_head[panel_index].astype(jnp.float32) - pulled).astype(jnp.bfloat16)
        upper_list[panel_index] = reduce_row(
            jnp.dot(backward_inverse[panel_index], shifted, preferred_element_type=jnp.float32)
        )
    upper_head = jnp.stack(upper_list)
    panel_cols = upper_head.shape[1]
    flat_back = backward_slab.reshape(backward_slab.shape[0], panels * panel_cols)
    flat_upper = upper_head.reshape(panels * panel_cols, classes)
    upper_update = lax.psum_scatter(
        with_layout_constraint(
            jnp.dot(flat_back, flat_upper, preferred_element_type=jnp.float32).astype(jnp.bfloat16),
            Layout(major_to_minor=(0, 1)),
        ),
        "col",
        scatter_dimension=0,
        tiled=True,
    ).astype(jnp.float32)
    upper_tail = (backward_tail.astype(jnp.float32) - upper_update).astype(jnp.bfloat16)
    return (lower_head, lower_tail, upper_head, upper_tail)


def solution(mesh):
    in_specs = (
        P(None, "col", None),
        P(("col", "row"), None),
        P(None, "col", "row"),
        P(None, "row", "col"),
        P(None, "row", "col"),
        P(None, "row", None),
        P(("row", "col"), None),
        P(None, "col", "row"),
        P(None, "row", "col"),
        P("row", None, "col"),
    )
    out_specs = (
        P(None, "row", None),
        P(("col", "row"), None),
        P(None, "col", None),
        P(("row", "col"), None),
    )
    return jax.shard_map(local, mesh=mesh, in_specs=in_specs, out_specs=out_specs, check_vma=False)
```

```python
import jax
import jax.numpy as jnp
from jax import lax
from jax.experimental.layout import Layout, with_layout_constraint
from jax.sharding import PartitionSpec as P

ROW_INNER = 2
COL_INNER = 4


def shift_pairs(n, inner, sub, d):
    outer = n // inner
    pairs = []
    for o in range(outer):
        for i in range(inner):
            if sub == "inner":
                pairs.append((o * inner + i, o * inner + (i + d) % inner))
            else:
                pairs.append((o * inner + i, ((o + d) % outer) * inner + i))
    return pairs


def sub_index(axis, inner, sub):
    a = lax.axis_index(axis)
    return a % inner if sub == "inner" else a // inner


def sub_size(n, inner, sub):
    return inner if sub == "inner" else n // inner


def ar_direct(v, axis, n, inner, sub):
    size = sub_size(n, inner, sub)
    acc = v.astype(jnp.float32)
    send = v.astype(jnp.bfloat16)
    for d in range(1, size):
        acc = acc + lax.ppermute(send, axis, shift_pairs(n, inner, sub, d)).astype(jnp.float32)
    return acc


def rs_direct(v, axis, n, inner, sub):
    size = sub_size(n, inner, sub)
    me = sub_index(axis, inner, sub)
    pieces = v.reshape(size, v.shape[0] // size, v.shape[1])
    acc = lax.dynamic_index_in_dim(pieces, me, 0, keepdims=False).astype(jnp.float32)
    for d in range(1, size):
        sel = lax.dynamic_index_in_dim(pieces, (me + d) % size, 0, keepdims=False)
        acc = acc + lax.ppermute(
            sel.astype(jnp.bfloat16), axis, shift_pairs(n, inner, sub, d)
        ).astype(jnp.float32)
    return acc


def ag_direct(p, axis, n, inner, sub):
    size = sub_size(n, inner, sub)
    me = sub_index(axis, inner, sub)
    got = [p] + [lax.ppermute(p, axis, shift_pairs(n, inner, sub, -d)) for d in range(1, size)]
    stacked = jnp.roll(jnp.stack(got), me, axis=0)
    return stacked.reshape(size * p.shape[0], p.shape[1])


def rs_hier(value, axis, inner):
    n = lax.axis_size(axis)
    outer = n // inner
    rows = value.shape[0] // n
    me_in = sub_index(axis, inner, "inner")
    me_out = sub_index(axis, inner, "outer")
    grid = value.reshape(outer, inner, rows, value.shape[1])
    acc = lax.dynamic_index_in_dim(grid, me_in, 1, keepdims=False).astype(jnp.float32)
    for d in range(1, inner):
        sel = lax.dynamic_index_in_dim(grid, (me_in + d) % inner, 1, keepdims=False)
        acc = acc + lax.ppermute(sel, axis, shift_pairs(n, inner, "inner", d)).astype(jnp.float32)
    half = acc.astype(jnp.bfloat16)
    total = lax.dynamic_index_in_dim(acc, me_out, 0, keepdims=False)
    for d in range(1, outer):
        sel = lax.dynamic_index_in_dim(half, (me_out + d) % outer, 0, keepdims=False)
        total = total + lax.ppermute(sel, axis, shift_pairs(n, inner, "outer", d)).astype(jnp.float32)
    return total


def allreduce(value, axis, inner):
    n = lax.axis_size(axis)
    piece = rs_direct(value.astype(jnp.bfloat16), axis, n, inner, "inner")
    piece = ar_direct(piece.astype(jnp.bfloat16), axis, n, inner, "outer").astype(jnp.bfloat16)
    return ag_direct(piece, axis, n, inner, "inner")


def reduce_row(value):
    return allreduce(value, "row", ROW_INNER)


def allreduce_a2a(value, axis):
    n = lax.axis_size(axis)
    m, k = value.shape
    spread = lax.all_to_all(value.astype(jnp.bfloat16), axis, 0, 0, tiled=True)
    piece = spread.reshape(n, m // n, k).astype(jnp.float32).sum(0).astype(jnp.bfloat16)
    copies = jnp.broadcast_to(piece[None], (n, m // n, k)).reshape(m, k)
    return lax.all_to_all(copies, axis, 0, 0, tiled=True)


def reduce_col(value):
    return allreduce_a2a(value, "col")


def leading_dot(left, right):
    return lax.dot_general(
        left, right, (((0,), (0,)), ((), ())), preferred_element_type=jnp.float32
    )


def local(
    forward_head,
    forward_tail,
    forward_inverse,
    forward_coupling,
    forward_slab,
    backward_head,
    backward_tail,
    backward_inverse,
    backward_coupling,
    backward_slab,
):
    classes = forward_head.shape[2]
    panels = forward_head.shape[0]
    lower_list = []
    for panel_index in range(panels):
        if panel_index == 0:
            adjusted = forward_head[0]
        else:
            summed = leading_dot(
                forward_coupling[panel_index * (panel_index - 1) // 2], lower_list[0]
            )
            for earlier in range(1, panel_index):
                summed = summed + leading_dot(
                    forward_coupling[panel_index * (panel_index - 1) // 2 + earlier],
                    lower_list[earlier],
                )
            coupling = reduce_row(summed).astype(jnp.float32)
            adjusted = (forward_head[panel_index].astype(jnp.float32) - coupling).astype(
                jnp.bfloat16
            )
        lower_list.append(reduce_col(leading_dot(forward_inverse[panel_index], adjusted)))
    lower_head = jnp.stack(lower_list)
    panel_rows = lower_head.shape[1]
    flat_lower = lower_head.reshape(panels * panel_rows, classes)
    flat_slab = forward_slab.reshape(panels * panel_rows, forward_slab.shape[2])
    lower_partial = with_layout_constraint(
        leading_dot(flat_slab, flat_lower).astype(jnp.bfloat16), Layout(major_to_minor=(0, 1))
    )
    lower_update = rs_hier(lower_partial, "row", ROW_INNER)
    lower_tail = (forward_tail.astype(jnp.float32) - lower_update).astype(jnp.bfloat16)
    upper_list = [None] * panels
    for panel_index in reversed(range(panels)):
        if panel_index == panels - 1:
            shifted = backward_head[panel_index]
        else:
            summed = None
            for later_panel in range(panel_index + 1, panels):
                block = backward_coupling[later_panel * (later_panel - 1) // 2 + panel_index]
                product = jnp.dot(
                    block, upper_list[later_panel], preferred_element_type=jnp.float32
                )
                summed = product if summed is None else summed + product
            pulled = reduce_col(summed).astype(jnp.float32)
            shifted = (backward_head[panel_index].astype(jnp.float32) - pulled).astype(jnp.bfloat16)
        upper_list[panel_index] = reduce_row(
            jnp.dot(backward_inverse[panel_index], shifted, preferred_element_type=jnp.float32)
        )
    upper_head = jnp.stack(upper_list)
    panel_cols = upper_head.shape[1]
    flat_back = backward_slab.reshape(backward_slab.shape[0], panels * panel_cols)
    flat_upper = upper_head.reshape(panels * panel_cols, classes)
    upper_update = lax.psum_scatter(
        with_layout_constraint(
            jnp.dot(flat_back, flat_upper, preferred_element_type=jnp.float32).astype(jnp.bfloat16),
            Layout(major_to_minor=(0, 1)),
        ),
        "col",
        scatter_dimension=0,
        tiled=True,
    ).astype(jnp.float32)
    upper_tail = (backward_tail.astype(jnp.float32) - upper_update).astype(jnp.bfloat16)
    return (lower_head, lower_tail, upper_head, upper_tail)


def solution(mesh):
    in_specs = (
        P(None, "col", None),
        P(("col", "row"), None),
        P(None, "col", "row"),
        P(None, "row", "col"),
        P(None, "row", "col"),
        P(None, "row", None),
        P(("row", "col"), None),
        P(None, "col", "row"),
        P(None, "row", "col"),
        P("row", None, "col"),
    )
    out_specs = (
        P(None, "row", None),
        P(("col", "row"), None),
        P(None, "col", None),
        P(("row", "col"), None),
    )
    return jax.shard_map(local, mesh=mesh, in_specs=in_specs, out_specs=out_specs, check_vma=False)
```

```python
import jax
import jax.numpy as jnp
from jax import lax
from jax.experimental.layout import Layout, with_layout_constraint
from jax.sharding import PartitionSpec as P

ROW_INNER = 2
COL_INNER = 4


def shift_pairs(n, inner, sub, d):
    outer = n // inner
    pairs = []
    for o in range(outer):
        for i in range(inner):
            if sub == "inner":
                pairs.append((o * inner + i, o * inner + (i + d) % inner))
            else:
                pairs.append((o * inner + i, ((o + d) % outer) * inner + i))
    return pairs


def sub_index(axis, inner, sub):
    a = lax.axis_index(axis)
    return a % inner if sub == "inner" else a // inner


def sub_size(n, inner, sub):
    return inner if sub == "inner" else n // inner


def ar_direct(v, axis, n, inner, sub):
    size = sub_size(n, inner, sub)
    acc = v.astype(jnp.float32)
    send = v.astype(jnp.bfloat16)
    for d in range(1, size):
        acc = acc + lax.ppermute(send, axis, shift_pairs(n, inner, sub, d)).astype(jnp.float32)
    return acc


def rs_direct(v, axis, n, inner, sub):
    size = sub_size(n, inner, sub)
    me = sub_index(axis, inner, sub)
    pieces = v.reshape(size, v.shape[0] // size, v.shape[1])
    acc = lax.dynamic_index_in_dim(pieces, me, 0, keepdims=False).astype(jnp.float32)
    for d in range(1, size):
        sel = lax.dynamic_index_in_dim(pieces, (me + d) % size, 0, keepdims=False)
        acc = acc + lax.ppermute(
            sel.astype(jnp.bfloat16), axis, shift_pairs(n, inner, sub, d)
        ).astype(jnp.float32)
    return acc


def ag_direct(p, axis, n, inner, sub):
    size = sub_size(n, inner, sub)
    me = sub_index(axis, inner, sub)
    got = [p] + [lax.ppermute(p, axis, shift_pairs(n, inner, sub, -d)) for d in range(1, size)]
    stacked = jnp.roll(jnp.stack(got), me, axis=0)
    return stacked.reshape(size * p.shape[0], p.shape[1])


def rs_hier(value, axis, inner):
    n = lax.axis_size(axis)
    outer = n // inner
    rows = value.shape[0] // n
    me_in = sub_index(axis, inner, "inner")
    me_out = sub_index(axis, inner, "outer")
    grid = value.reshape(outer, inner, rows, value.shape[1])
    acc = lax.dynamic_index_in_dim(grid, me_in, 1, keepdims=False).astype(jnp.float32)
    for d in range(1, inner):
        sel = lax.dynamic_index_in_dim(grid, (me_in + d) % inner, 1, keepdims=False)
        acc = acc + lax.ppermute(sel, axis, shift_pairs(n, inner, "inner", d)).astype(jnp.float32)
    half = acc.astype(jnp.bfloat16)
    total = lax.dynamic_index_in_dim(acc, me_out, 0, keepdims=False)
    for d in range(1, outer):
        sel = lax.dynamic_index_in_dim(half, (me_out + d) % outer, 0, keepdims=False)
        total = total + lax.ppermute(sel, axis, shift_pairs(n, inner, "outer", d)).astype(jnp.float32)
    return total


def allreduce(value, axis, inner):
    n = lax.axis_size(axis)
    piece = rs_direct(value.astype(jnp.bfloat16), axis, n, inner, "inner")
    piece = ar_direct(piece.astype(jnp.bfloat16), axis, n, inner, "outer").astype(jnp.bfloat16)
    return ag_direct(piece, axis, n, inner, "inner")


def reduce_row(value):
    return allreduce(value, "row", ROW_INNER)


def reduce_col(value):
    return allreduce(value, "col", COL_INNER)


def leading_dot(left, right):
    return lax.dot_general(
        left, right, (((0,), (0,)), ((), ())), preferred_element_type=jnp.float32
    )


def local(
    forward_head,
    forward_tail,
    forward_inverse,
    forward_coupling,
    forward_slab,
    backward_head,
    backward_tail,
    backward_inverse,
    backward_coupling,
    backward_slab,
):
    classes = forward_head.shape[2]
    panels = forward_head.shape[0]
    upper_list = [None] * panels
    lower_list = []
    for step in range(panels):
        panel_index = panels - 1 - step
        if panel_index == panels - 1:
            shifted = backward_head[panel_index]
        else:
            summed = None
            for later_panel in range(panel_index + 1, panels):
                block = backward_coupling[later_panel * (later_panel - 1) // 2 + panel_index]
                product = jnp.dot(
                    block, upper_list[later_panel], preferred_element_type=jnp.float32
                )
                summed = product if summed is None else summed + product
            pulled = reduce_col(summed).astype(jnp.float32)
            shifted = (backward_head[panel_index].astype(jnp.float32) - pulled).astype(jnp.bfloat16)
        upper_list[panel_index] = reduce_row(
            jnp.dot(backward_inverse[panel_index], shifted, preferred_element_type=jnp.float32)
        )

        panel_index = step
        if panel_index == 0:
            adjusted = forward_head[0]
        else:
            summed = leading_dot(
                forward_coupling[panel_index * (panel_index - 1) // 2], lower_list[0]
            )
            for earlier in range(1, panel_index):
                summed = summed + leading_dot(
                    forward_coupling[panel_index * (panel_index - 1) // 2 + earlier],
                    lower_list[earlier],
                )
            coupling = reduce_row(summed).astype(jnp.float32)
            adjusted = (forward_head[panel_index].astype(jnp.float32) - coupling).astype(
                jnp.bfloat16
            )
        lead = upper_list[panels - 1 - step]
        if step == panels - 1:
            upper_head = jnp.stack(upper_list)
            panel_cols = upper_head.shape[1]
            flat_back = backward_slab.reshape(backward_slab.shape[0], panels * panel_cols)
            flat_upper = upper_head.reshape(panels * panel_cols, classes)
            upper_partial = with_layout_constraint(
                jnp.dot(flat_back, flat_upper, preferred_element_type=jnp.float32).astype(
                    jnp.bfloat16
                ),
                Layout(major_to_minor=(0, 1)),
            )
            lead = upper_partial
        partial, _ = lax.optimization_barrier(
            (leading_dot(forward_inverse[panel_index], adjusted), lead)
        )
        lower_list.append(reduce_col(partial))
    lower_head = jnp.stack(lower_list)
    panel_rows = lower_head.shape[1]
    flat_lower = lower_head.reshape(panels * panel_rows, classes)
    flat_slab = forward_slab.reshape(panels * panel_rows, forward_slab.shape[2])
    lower_partial = with_layout_constraint(
        leading_dot(flat_slab, flat_lower).astype(jnp.bfloat16), Layout(major_to_minor=(0, 1))
    )
    lower_update = rs_hier(lower_partial, "row", ROW_INNER)
    lower_tail = (forward_tail.astype(jnp.float32) - lower_update).astype(jnp.bfloat16)
    upper_update = lax.psum_scatter(
        upper_partial,
        "col",
        scatter_dimension=0,
        tiled=True,
    ).astype(jnp.float32)
    upper_tail = (backward_tail.astype(jnp.float32) - upper_update).astype(jnp.bfloat16)
    return (lower_head, lower_tail, upper_head, upper_tail)


def solution(mesh):
    in_specs = (
        P(None, "col", None),
        P(("col", "row"), None),
        P(None, "col", "row"),
        P(None, "row", "col"),
        P(None, "row", "col"),
        P(None, "row", None),
        P(("row", "col"), None),
        P(None, "col", "row"),
        P(None, "row", "col"),
        P("row", None, "col"),
    )
    out_specs = (
        P(None, "row", None),
        P(("col", "row"), None),
        P(None, "col", None),
        P(("row", "col"), None),
    )
    return jax.shard_map(local, mesh=mesh, in_specs=in_specs, out_specs=out_specs, check_vma=False)
```

```python
import jax
import jax.numpy as jnp
from jax import lax
from jax.experimental.layout import Layout, with_layout_constraint
from jax.sharding import PartitionSpec as P

ROW_INNER = 2
COL_INNER = 4


def shift_pairs(n, inner, sub, d):
    outer = n // inner
    pairs = []
    for o in range(outer):
        for i in range(inner):
            if sub == "inner":
                pairs.append((o * inner + i, o * inner + (i + d) % inner))
            else:
                pairs.append((o * inner + i, ((o + d) % outer) * inner + i))
    return pairs


def sub_index(axis, inner, sub):
    a = lax.axis_index(axis)
    return a % inner if sub == "inner" else a // inner


def sub_size(n, inner, sub):
    return inner if sub == "inner" else n // inner


def ar_direct(v, axis, n, inner, sub):
    size = sub_size(n, inner, sub)
    acc = v.astype(jnp.float32)
    send = v.astype(jnp.bfloat16)
    for d in range(1, size):
        acc = acc + lax.ppermute(send, axis, shift_pairs(n, inner, sub, d)).astype(jnp.float32)
    return acc


def rs_direct(v, axis, n, inner, sub):
    size = sub_size(n, inner, sub)
    me = sub_index(axis, inner, sub)
    pieces = v.reshape(size, v.shape[0] // size, v.shape[1])
    acc = lax.dynamic_index_in_dim(pieces, me, 0, keepdims=False).astype(jnp.float32)
    for d in range(1, size):
        sel = lax.dynamic_index_in_dim(pieces, (me + d) % size, 0, keepdims=False)
        acc = acc + lax.ppermute(
            sel.astype(jnp.bfloat16), axis, shift_pairs(n, inner, sub, d)
        ).astype(jnp.float32)
    return acc


def ag_direct(p, axis, n, inner, sub):
    size = sub_size(n, inner, sub)
    me = sub_index(axis, inner, sub)
    got = [p] + [lax.ppermute(p, axis, shift_pairs(n, inner, sub, -d)) for d in range(1, size)]
    stacked = jnp.roll(jnp.stack(got), me, axis=0)
    return stacked.reshape(size * p.shape[0], p.shape[1])


def rs_hier(value, axis, inner):
    n = lax.axis_size(axis)
    outer = n // inner
    rows = value.shape[0] // n
    me_in = sub_index(axis, inner, "inner")
    me_out = sub_index(axis, inner, "outer")
    grid = value.reshape(outer, inner, rows, value.shape[1])
    acc = lax.dynamic_index_in_dim(grid, me_in, 1, keepdims=False).astype(jnp.float32)
    for d in range(1, inner):
        sel = lax.dynamic_index_in_dim(grid, (me_in + d) % inner, 1, keepdims=False)
        acc = acc + lax.ppermute(sel, axis, shift_pairs(n, inner, "inner", d)).astype(jnp.float32)
    half = acc.astype(jnp.bfloat16)
    total = lax.dynamic_index_in_dim(acc, me_out, 0, keepdims=False)
    for d in range(1, outer):
        sel = lax.dynamic_index_in_dim(half, (me_out + d) % outer, 0, keepdims=False)
        total = total + lax.ppermute(sel, axis, shift_pairs(n, inner, "outer", d)).astype(jnp.float32)
    return total


def allreduce(value, axis, inner):
    n = lax.axis_size(axis)
    piece = rs_direct(value.astype(jnp.bfloat16), axis, n, inner, "inner")
    piece = ar_direct(piece.astype(jnp.bfloat16), axis, n, inner, "outer").astype(jnp.bfloat16)
    return ag_direct(piece, axis, n, inner, "inner")


def reduce_row(value):
    return allreduce(value, "row", ROW_INNER)


def reduce_col(value):
    return allreduce(value, "col", COL_INNER)


def leading_dot(left, right):
    return lax.dot_general(
        left, right, (((0,), (0,)), ((), ())), preferred_element_type=jnp.float32
    )


def local(
    forward_head,
    forward_tail,
    forward_inverse,
    forward_coupling,
    forward_slab,
    backward_head,
    backward_tail,
    backward_inverse,
    backward_coupling,
    backward_slab,
):
    classes = forward_head.shape[2]
    panels = forward_head.shape[0]
    upper_list = [None] * panels
    lower_list = []
    for step in range(panels):
        panel_index = panels - 1 - step
        if panel_index == panels - 1:
            shifted = backward_head[panel_index]
        else:
            summed = None
            for later_panel in range(panel_index + 1, panels):
                block = backward_coupling[later_panel * (later_panel - 1) // 2 + panel_index]
                product = jnp.dot(
                    block, upper_list[later_panel], preferred_element_type=jnp.float32
                )
                summed = product if summed is None else summed + product
            pulled = reduce_col(summed).astype(jnp.float32)
            shifted = (backward_head[panel_index].astype(jnp.float32) - pulled).astype(jnp.bfloat16)
        upper_list[panel_index] = reduce_row(
            jnp.dot(backward_inverse[panel_index], shifted, preferred_element_type=jnp.float32)
        )

        panel_index = step
        if panel_index == 0:
            adjusted = forward_head[0]
        else:
            summed = leading_dot(
                forward_coupling[panel_index * (panel_index - 1) // 2], lower_list[0]
            )
            for earlier in range(1, panel_index):
                summed = summed + leading_dot(
                    forward_coupling[panel_index * (panel_index - 1) // 2 + earlier],
                    lower_list[earlier],
                )
            coupling = reduce_row(summed).astype(jnp.float32)
            adjusted = (forward_head[panel_index].astype(jnp.float32) - coupling).astype(
                jnp.bfloat16
            )
        lead = upper_list[panels - 1 - step]
        if step == panels - 1:
            upper_head = jnp.stack(upper_list)
            panel_cols = upper_head.shape[1]
            flat_back = backward_slab.reshape(backward_slab.shape[0], panels * panel_cols)
            flat_upper = upper_head.reshape(panels * panel_cols, classes)
            upper_partial = with_layout_constraint(
                jnp.dot(flat_back, flat_upper, preferred_element_type=jnp.float32).astype(
                    jnp.bfloat16
                ),
                Layout(major_to_minor=(0, 1)),
            )
            lead = upper_partial
        partial, _ = lax.optimization_barrier(
            (leading_dot(forward_inverse[panel_index], adjusted), lead)
        )
        lower_list.append(reduce_col(partial))
    lower_head = jnp.stack(lower_list)
    panel_rows = lower_head.shape[1]
    early = panels - 1
    early_lower = lower_head[:early].reshape(early * panel_rows, classes)
    early_slab = forward_slab[:early].reshape(early * panel_rows, forward_slab.shape[2])
    early_partial = with_layout_constraint(
        leading_dot(early_slab, early_lower), Layout(major_to_minor=(0, 1))
    )
    lower_partial = with_layout_constraint(
        (early_partial + leading_dot(forward_slab[early], lower_head[early])).astype(jnp.bfloat16),
        Layout(major_to_minor=(0, 1)),
    )
    lower_update = rs_hier(lower_partial, "row", ROW_INNER)
    lower_tail = (forward_tail.astype(jnp.float32) - lower_update).astype(jnp.bfloat16)
    upper_update = lax.psum_scatter(
        upper_partial,
        "col",
        scatter_dimension=0,
        tiled=True,
    ).astype(jnp.float32)
    upper_tail = (backward_tail.astype(jnp.float32) - upper_update).astype(jnp.bfloat16)
    return (lower_head, lower_tail, upper_head, upper_tail)


def solution(mesh):
    in_specs = (
        P(None, "col", None),
        P(("col", "row"), None),
        P(None, "col", "row"),
        P(None, "row", "col"),
        P(None, "row", "col"),
        P(None, "row", None),
        P(("row", "col"), None),
        P(None, "col", "row"),
        P(None, "row", "col"),
        P("row", None, "col"),
    )
    out_specs = (
        P(None, "row", None),
        P(("col", "row"), None),
        P(None, "col", None),
        P(("row", "col"), None),
    )
    return jax.shard_map(local, mesh=mesh, in_specs=in_specs, out_specs=out_specs, check_vma=False)
```

```python
import jax
import jax.numpy as jnp
from jax import lax
from jax.experimental.layout import Layout, with_layout_constraint
from jax.sharding import PartitionSpec as P

ROW_INNER = 2
COL_INNER = 4


def shift_pairs(n, inner, sub, d):
    outer = n // inner
    pairs = []
    for o in range(outer):
        for i in range(inner):
            if sub == "inner":
                pairs.append((o * inner + i, o * inner + (i + d) % inner))
            else:
                pairs.append((o * inner + i, ((o + d) % outer) * inner + i))
    return pairs


def sub_index(axis, inner, sub):
    a = lax.axis_index(axis)
    return a % inner if sub == "inner" else a // inner


def sub_size(n, inner, sub):
    return inner if sub == "inner" else n // inner


def ar_direct(v, axis, n, inner, sub):
    size = sub_size(n, inner, sub)
    acc = v.astype(jnp.float32)
    send = v.astype(jnp.bfloat16)
    for d in range(1, size):
        acc = acc + lax.ppermute(send, axis, shift_pairs(n, inner, sub, d)).astype(jnp.float32)
    return acc


def rs_direct(v, axis, n, inner, sub):
    size = sub_size(n, inner, sub)
    me = sub_index(axis, inner, sub)
    pieces = v.reshape(size, v.shape[0] // size, v.shape[1])
    acc = lax.dynamic_index_in_dim(pieces, me, 0, keepdims=False).astype(jnp.float32)
    for d in range(1, size):
        sel = lax.dynamic_index_in_dim(pieces, (me + d) % size, 0, keepdims=False)
        acc = acc + lax.ppermute(
            sel.astype(jnp.bfloat16), axis, shift_pairs(n, inner, sub, d)
        ).astype(jnp.float32)
    return acc


def ag_direct(p, axis, n, inner, sub):
    size = sub_size(n, inner, sub)
    me = sub_index(axis, inner, sub)
    got = [p] + [lax.ppermute(p, axis, shift_pairs(n, inner, sub, -d)) for d in range(1, size)]
    stacked = jnp.roll(jnp.stack(got), me, axis=0)
    return stacked.reshape(size * p.shape[0], p.shape[1])


def rs_hier(value, axis, inner):
    n = lax.axis_size(axis)
    outer = n // inner
    rows = value.shape[0] // n
    me_in = sub_index(axis, inner, "inner")
    me_out = sub_index(axis, inner, "outer")
    grid = value.reshape(outer, inner, rows, value.shape[1])
    received = None
    for d in range(1, inner):
        sel = lax.dynamic_index_in_dim(grid, (me_in + d) % inner, 1, keepdims=False)
        got = lax.ppermute(sel, axis, shift_pairs(n, inner, "inner", d)).astype(jnp.float32)
        received = got if received is None else received + got
    acc = lax.dynamic_index_in_dim(grid, me_in, 1, keepdims=False).astype(jnp.float32) + received
    half = acc.astype(jnp.bfloat16)
    total = lax.dynamic_index_in_dim(
        lax.dynamic_index_in_dim(grid, me_in, 1, keepdims=False), me_out, 0, keepdims=False
    ).astype(jnp.float32) + lax.dynamic_index_in_dim(received, me_out, 0, keepdims=False)
    for d in range(1, outer):
        sel = lax.dynamic_index_in_dim(half, (me_out + d) % outer, 0, keepdims=False)
        total = total + lax.ppermute(sel, axis, shift_pairs(n, inner, "outer", d)).astype(jnp.float32)
    return total


def allreduce(value, axis, inner):
    n = lax.axis_size(axis)
    piece = rs_direct(value.astype(jnp.bfloat16), axis, n, inner, "inner")
    piece = ar_direct(piece.astype(jnp.bfloat16), axis, n, inner, "outer").astype(jnp.bfloat16)
    return ag_direct(piece, axis, n, inner, "inner")


def reduce_row(value):
    return allreduce(value, "row", ROW_INNER)


def reduce_col(value):
    return allreduce(value, "col", COL_INNER)


def leading_dot(left, right):
    return lax.dot_general(
        left, right, (((0,), (0,)), ((), ())), preferred_element_type=jnp.float32
    )


def local(
    forward_head,
    forward_tail,
    forward_inverse,
    forward_coupling,
    forward_slab,
    backward_head,
    backward_tail,
    backward_inverse,
    backward_coupling,
    backward_slab,
):
    classes = forward_head.shape[2]
    panels = forward_head.shape[0]
    upper_list = [None] * panels
    lower_list = []
    for step in range(panels):
        panel_index = panels - 1 - step
        if panel_index == panels - 1:
            shifted = backward_head[panel_index]
        else:
            summed = None
            for later_panel in range(panel_index + 1, panels):
                block = backward_coupling[later_panel * (later_panel - 1) // 2 + panel_index]
                product = jnp.dot(
                    block, upper_list[later_panel], preferred_element_type=jnp.float32
                )
                summed = product if summed is None else summed + product
            pulled = reduce_col(summed).astype(jnp.float32)
            shifted = (backward_head[panel_index].astype(jnp.float32) - pulled).astype(jnp.bfloat16)
        upper_list[panel_index] = reduce_row(
            jnp.dot(backward_inverse[panel_index], shifted, preferred_element_type=jnp.float32)
        )

        panel_index = step
        if panel_index == 0:
            adjusted = forward_head[0]
        else:
            summed = leading_dot(
                forward_coupling[panel_index * (panel_index - 1) // 2], lower_list[0]
            )
            for earlier in range(1, panel_index):
                summed = summed + leading_dot(
                    forward_coupling[panel_index * (panel_index - 1) // 2 + earlier],
                    lower_list[earlier],
                )
            coupling = reduce_row(summed).astype(jnp.float32)
            adjusted = (forward_head[panel_index].astype(jnp.float32) - coupling).astype(
                jnp.bfloat16
            )
        lead = upper_list[panels - 1 - step]
        if step == panels - 1:
            upper_head = jnp.stack(upper_list)
            panel_cols = upper_head.shape[1]
            flat_back = backward_slab.reshape(backward_slab.shape[0], panels * panel_cols)
            flat_upper = upper_head.reshape(panels * panel_cols, classes)
            upper_partial = with_layout_constraint(
                jnp.dot(flat_back, flat_upper, preferred_element_type=jnp.float32).astype(
                    jnp.bfloat16
                ),
                Layout(major_to_minor=(0, 1)),
            )
            lead = upper_partial
        partial, _ = lax.optimization_barrier(
            (leading_dot(forward_inverse[panel_index], adjusted), lead)
        )
        lower_list.append(reduce_col(partial))
    lower_head = jnp.stack(lower_list)
    panel_rows = lower_head.shape[1]
    early = panels - 1
    early_slab = forward_slab[:early].reshape(early * panel_rows, forward_slab.shape[2])
    split = 512 if classes > 512 else classes
    updates = []
    for lo, hi in ((0, split), (split, classes)):
        if hi <= lo:
            continue
        part = lower_head[:, :, lo:hi]
        early_partial = with_layout_constraint(
            leading_dot(early_slab, part[:early].reshape(early * panel_rows, hi - lo)),
            Layout(major_to_minor=(0, 1)),
        )
        lower_partial = with_layout_constraint(
            (early_partial + leading_dot(forward_slab[early], part[early])).astype(jnp.bfloat16),
            Layout(major_to_minor=(0, 1)),
        )
        updates.append(rs_hier(lower_partial, "row", ROW_INNER))
    lower_update = jnp.concatenate(updates, axis=1)
    lower_tail = (forward_tail.astype(jnp.float32) - lower_update).astype(jnp.bfloat16)
    upper_update = lax.psum_scatter(
        upper_partial,
        "col",
        scatter_dimension=0,
        tiled=True,
    ).astype(jnp.float32)
    upper_tail = (backward_tail.astype(jnp.float32) - upper_update).astype(jnp.bfloat16)
    return (lower_head, lower_tail, upper_head, upper_tail)


def solution(mesh):
    in_specs = (
        P(None, "col", None),
        P(("col", "row"), None),
        P(None, "col", "row"),
        P(None, "row", "col"),
        P(None, "row", "col"),
        P(None, "row", None),
        P(("row", "col"), None),
        P(None, "col", "row"),
        P(None, "row", "col"),
        P("row", None, "col"),
    )
    out_specs = (
        P(None, "row", None),
        P(("col", "row"), None),
        P(None, "col", None),
        P(("row", "col"), None),
    )
    return jax.shard_map(local, mesh=mesh, in_specs=in_specs, out_specs=out_specs, check_vma=False)
```

```python
import jax
import jax.numpy as jnp
from jax import lax
from jax.experimental.layout import Layout, with_layout_constraint
from jax.sharding import PartitionSpec as P

ROW_INNER = 2
COL_INNER = 4


def shift_pairs(n, inner, sub, d):
    outer = n // inner
    pairs = []
    for o in range(outer):
        for i in range(inner):
            if sub == "inner":
                pairs.append((o * inner + i, o * inner + (i + d) % inner))
            else:
                pairs.append((o * inner + i, ((o + d) % outer) * inner + i))
    return pairs


def sub_index(axis, inner, sub):
    a = lax.axis_index(axis)
    return a % inner if sub == "inner" else a // inner


def sub_size(n, inner, sub):
    return inner if sub == "inner" else n // inner


def ar_direct(v, axis, n, inner, sub):
    size = sub_size(n, inner, sub)
    acc = v.astype(jnp.float32)
    send = v.astype(jnp.bfloat16)
    for d in range(1, size):
        acc = acc + lax.ppermute(send, axis, shift_pairs(n, inner, sub, d)).astype(jnp.float32)
    return acc


def rs_direct(v, axis, n, inner, sub):
    size = sub_size(n, inner, sub)
    me = sub_index(axis, inner, sub)
    pieces = v.reshape(size, v.shape[0] // size, v.shape[1])
    acc = lax.dynamic_index_in_dim(pieces, me, 0, keepdims=False).astype(jnp.float32)
    for d in range(1, size):
        sel = lax.dynamic_index_in_dim(pieces, (me + d) % size, 0, keepdims=False)
        acc = acc + lax.ppermute(
            sel.astype(jnp.bfloat16), axis, shift_pairs(n, inner, sub, d)
        ).astype(jnp.float32)
    return acc


def ag_direct(p, axis, n, inner, sub):
    size = sub_size(n, inner, sub)
    me = sub_index(axis, inner, sub)
    got = [p] + [lax.ppermute(p, axis, shift_pairs(n, inner, sub, -d)) for d in range(1, size)]
    stacked = jnp.roll(jnp.stack(got), me, axis=0)
    return stacked.reshape(size * p.shape[0], p.shape[1])


def rs_hier(value, axis, inner):
    n = lax.axis_size(axis)
    outer = n // inner
    rows = value.shape[0] // n
    me_in = sub_index(axis, inner, "inner")
    me_out = sub_index(axis, inner, "outer")
    grid = value.reshape(outer, inner, rows, value.shape[1])
    received = None
    for d in range(1, inner):
        sel = lax.dynamic_index_in_dim(grid, (me_in + d) % inner, 1, keepdims=False)
        got = lax.ppermute(sel, axis, shift_pairs(n, inner, "inner", d)).astype(jnp.float32)
        received = got if received is None else received + got
    acc = lax.dynamic_index_in_dim(grid, me_in, 1, keepdims=False).astype(jnp.float32) + received
    half = acc.astype(jnp.bfloat16)
    total = lax.dynamic_index_in_dim(
        lax.dynamic_index_in_dim(grid, me_in, 1, keepdims=False), me_out, 0, keepdims=False
    ).astype(jnp.float32) + lax.dynamic_index_in_dim(received, me_out, 0, keepdims=False)
    for d in range(1, outer):
        sel = lax.dynamic_index_in_dim(half, (me_out + d) % outer, 0, keepdims=False)
        total = total + lax.ppermute(sel, axis, shift_pairs(n, inner, "outer", d)).astype(jnp.float32)
    return total


def allreduce(value, axis, inner, hold=None):
    n = lax.axis_size(axis)
    piece = rs_direct(value.astype(jnp.bfloat16), axis, n, inner, "inner")
    piece = ar_direct(piece.astype(jnp.bfloat16), axis, n, inner, "outer").astype(jnp.bfloat16)
    if hold is not None:
        piece, _ = lax.optimization_barrier((piece, hold))
    return ag_direct(piece, axis, n, inner, "inner")


def reduce_row(value):
    return allreduce(value, "row", ROW_INNER)


def reduce_col(value, hold=None):
    return allreduce(value, "col", COL_INNER, hold)


def leading_dot(left, right):
    return lax.dot_general(
        left, right, (((0,), (0,)), ((), ())), preferred_element_type=jnp.float32
    )


def local(
    forward_head,
    forward_tail,
    forward_inverse,
    forward_coupling,
    forward_slab,
    backward_head,
    backward_tail,
    backward_inverse,
    backward_coupling,
    backward_slab,
):
    classes = forward_head.shape[2]
    panels = forward_head.shape[0]
    upper_list = [None] * panels
    lower_list = []
    for step in range(panels):
        panel_index = panels - 1 - step
        if panel_index == panels - 1:
            shifted = backward_head[panel_index]
        else:
            summed = None
            for later_panel in range(panel_index + 1, panels):
                block = backward_coupling[later_panel * (later_panel - 1) // 2 + panel_index]
                product = jnp.dot(
                    block, upper_list[later_panel], preferred_element_type=jnp.float32
                )
                summed = product if summed is None else summed + product
            pulled = reduce_col(summed).astype(jnp.float32)
            shifted = (backward_head[panel_index].astype(jnp.float32) - pulled).astype(jnp.bfloat16)
        upper_list[panel_index] = reduce_row(
            jnp.dot(backward_inverse[panel_index], shifted, preferred_element_type=jnp.float32)
        )

        panel_index = step
        if panel_index == 0:
            adjusted = forward_head[0]
        else:
            summed = leading_dot(
                forward_coupling[panel_index * (panel_index - 1) // 2], lower_list[0]
            )
            for earlier in range(1, panel_index):
                summed = summed + leading_dot(
                    forward_coupling[panel_index * (panel_index - 1) // 2 + earlier],
                    lower_list[earlier],
                )
            coupling = reduce_row(summed).astype(jnp.float32)
            adjusted = (forward_head[panel_index].astype(jnp.float32) - coupling).astype(
                jnp.bfloat16
            )
        lead = upper_list[panels - 1 - step]
        if step == panels - 1:
            upper_head = jnp.stack(upper_list)
            panel_cols = upper_head.shape[1]
            flat_back = backward_slab.reshape(backward_slab.shape[0], panels * panel_cols)
            flat_upper = upper_head.reshape(panels * panel_cols, classes)
            upper_partial = with_layout_constraint(
                jnp.dot(flat_back, flat_upper, preferred_element_type=jnp.float32).astype(
                    jnp.bfloat16
                ),
                Layout(major_to_minor=(0, 1)),
            )
        partial, _ = lax.optimization_barrier(
            (leading_dot(forward_inverse[panel_index], adjusted), lead)
        )
        lower_list.append(reduce_col(partial, upper_partial if step == panels - 1 else None))
    lower_head = jnp.stack(lower_list)
    panel_rows = lower_head.shape[1]
    early = panels - 1
    early_slab = forward_slab[:early].reshape(early * panel_rows, forward_slab.shape[2])
    split = 512 if classes > 512 else classes
    updates = []
    for lo, hi in ((0, split), (split, classes)):
        if hi <= lo:
            continue
        part = lower_head[:, :, lo:hi]
        early_partial = with_layout_constraint(
            leading_dot(early_slab, part[:early].reshape(early * panel_rows, hi - lo)),
            Layout(major_to_minor=(0, 1)),
        )
        lower_partial = with_layout_constraint(
            (early_partial + leading_dot(forward_slab[early], part[early])).astype(jnp.bfloat16),
            Layout(major_to_minor=(0, 1)),
        )
        updates.append(rs_hier(lower_partial, "row", ROW_INNER))
    lower_update = jnp.concatenate(updates, axis=1)
    lower_tail = (forward_tail.astype(jnp.float32) - lower_update).astype(jnp.bfloat16)
    upper_update = lax.psum_scatter(
        upper_partial,
        "col",
        scatter_dimension=0,
        tiled=True,
    ).astype(jnp.float32)
    upper_tail = (backward_tail.astype(jnp.float32) - upper_update).astype(jnp.bfloat16)
    return (lower_head, lower_tail, upper_head, upper_tail)


def solution(mesh):
    in_specs = (
        P(None, "col", None),
        P(("col", "row"), None),
        P(None, "col", "row"),
        P(None, "row", "col"),
        P(None, "row", "col"),
        P(None, "row", None),
        P(("row", "col"), None),
        P(None, "col", "row"),
        P(None, "row", "col"),
        P("row", None, "col"),
    )
    out_specs = (
        P(None, "row", None),
        P(("col", "row"), None),
        P(None, "col", None),
        P(("row", "col"), None),
    )
    return jax.shard_map(local, mesh=mesh, in_specs=in_specs, out_specs=out_specs, check_vma=False)
```

```python
import jax
import jax.numpy as jnp
from jax import lax
from jax.experimental.layout import Layout, with_layout_constraint
from jax.sharding import PartitionSpec as P

ROW_INNER = 2
COL_INNER = 4


def shift_pairs(n, inner, sub, d):
    outer = n // inner
    pairs = []
    for o in range(outer):
        for i in range(inner):
            if sub == "inner":
                pairs.append((o * inner + i, o * inner + (i + d) % inner))
            else:
                pairs.append((o * inner + i, ((o + d) % outer) * inner + i))
    return pairs


def sub_index(axis, inner, sub):
    a = lax.axis_index(axis)
    return a % inner if sub == "inner" else a // inner


def sub_size(n, inner, sub):
    return inner if sub == "inner" else n // inner


def ar_direct(v, axis, n, inner, sub):
    size = sub_size(n, inner, sub)
    acc = v.astype(jnp.float32)
    send = v.astype(jnp.bfloat16)
    for d in range(1, size):
        acc = acc + lax.ppermute(send, axis, shift_pairs(n, inner, sub, d)).astype(jnp.float32)
    return acc


def rs_direct(v, axis, n, inner, sub):
    size = sub_size(n, inner, sub)
    me = sub_index(axis, inner, sub)
    pieces = v.reshape(size, v.shape[0] // size, v.shape[1])
    acc = lax.dynamic_index_in_dim(pieces, me, 0, keepdims=False).astype(jnp.float32)
    for d in range(1, size):
        sel = lax.dynamic_index_in_dim(pieces, (me + d) % size, 0, keepdims=False)
        acc = acc + lax.ppermute(
            sel.astype(jnp.bfloat16), axis, shift_pairs(n, inner, sub, d)
        ).astype(jnp.float32)
    return acc


def ag_direct(p, axis, n, inner, sub):
    size = sub_size(n, inner, sub)
    me = sub_index(axis, inner, sub)
    got = [p] + [lax.ppermute(p, axis, shift_pairs(n, inner, sub, -d)) for d in range(1, size)]
    stacked = jnp.roll(jnp.stack(got), me, axis=0)
    return stacked.reshape(size * p.shape[0], p.shape[1])


def rs_hier(value, axis, inner):
    n = lax.axis_size(axis)
    outer = n // inner
    rows = value.shape[0] // n
    me_in = sub_index(axis, inner, "inner")
    me_out = sub_index(axis, inner, "outer")
    grid = value.reshape(outer, inner, rows, value.shape[1])
    received = None
    for d in range(1, inner):
        sel = lax.dynamic_index_in_dim(grid, (me_in + d) % inner, 1, keepdims=False)
        got = lax.ppermute(sel, axis, shift_pairs(n, inner, "inner", d)).astype(jnp.float32)
        received = got if received is None else received + got
    acc = lax.dynamic_index_in_dim(grid, me_in, 1, keepdims=False).astype(jnp.float32) + received
    half = acc.astype(jnp.bfloat16)
    total = lax.dynamic_index_in_dim(
        lax.dynamic_index_in_dim(grid, me_in, 1, keepdims=False), me_out, 0, keepdims=False
    ).astype(jnp.float32) + lax.dynamic_index_in_dim(received, me_out, 0, keepdims=False)
    for d in range(1, outer):
        sel = lax.dynamic_index_in_dim(half, (me_out + d) % outer, 0, keepdims=False)
        total = total + lax.ppermute(sel, axis, shift_pairs(n, inner, "outer", d)).astype(jnp.float32)
    return total


def allreduce(value, axis, inner, hold=None):
    n = lax.axis_size(axis)
    piece = rs_direct(value.astype(jnp.bfloat16), axis, n, inner, "inner")
    piece = ar_direct(piece.astype(jnp.bfloat16), axis, n, inner, "outer").astype(jnp.bfloat16)
    if hold is not None:
        piece, _ = lax.optimization_barrier((piece, hold))
    return ag_direct(piece, axis, n, inner, "inner")


def reduce_row(value):
    return allreduce(value, "row", ROW_INNER)


def reduce_col(value, hold=None):
    return allreduce(value, "col", COL_INNER, hold)


def leading_dot(left, right):
    return lax.dot_general(
        left, right, (((0,), (0,)), ((), ())), preferred_element_type=jnp.float32
    )


def local(
    forward_head,
    forward_tail,
    forward_inverse,
    forward_coupling,
    forward_slab,
    backward_head,
    backward_tail,
    backward_inverse,
    backward_coupling,
    backward_slab,
):
    classes = forward_head.shape[2]
    panels = forward_head.shape[0]
    upper_list = [None] * panels
    lower_list = []
    for step in range(panels):
        panel_index = panels - 1 - step
        if panel_index == panels - 1:
            shifted = backward_head[panel_index]
        else:
            summed = None
            for later_panel in range(panel_index + 1, panels):
                block = backward_coupling[later_panel * (later_panel - 1) // 2 + panel_index]
                product = jnp.dot(
                    block, upper_list[later_panel], preferred_element_type=jnp.float32
                )
                summed = product if summed is None else summed + product
            pulled = reduce_col(summed).astype(jnp.float32)
            shifted = (backward_head[panel_index].astype(jnp.float32) - pulled).astype(jnp.bfloat16)
        upper_list[panel_index] = reduce_row(
            jnp.dot(backward_inverse[panel_index], shifted, preferred_element_type=jnp.float32)
        )

        panel_index = step
        if panel_index == 0:
            adjusted = forward_head[0]
        else:
            summed = leading_dot(
                forward_coupling[panel_index * (panel_index - 1) // 2], lower_list[0]
            )
            for earlier in range(1, panel_index):
                summed = summed + leading_dot(
                    forward_coupling[panel_index * (panel_index - 1) // 2 + earlier],
                    lower_list[earlier],
                )
            coupling = reduce_row(summed).astype(jnp.float32)
            adjusted = (forward_head[panel_index].astype(jnp.float32) - coupling).astype(
                jnp.bfloat16
            )
        lead = upper_list[panels - 1 - step]
        if step == panels - 1:
            upper_head = jnp.stack(upper_list)
            panel_cols = upper_head.shape[1]
            flat_back = backward_slab.reshape(backward_slab.shape[0], panels * panel_cols)
            flat_upper = upper_head.reshape(panels * panel_cols, classes)
            upper_partial = with_layout_constraint(
                jnp.dot(flat_back, flat_upper, preferred_element_type=jnp.float32).astype(
                    jnp.bfloat16
                ),
                Layout(major_to_minor=(0, 1)),
            )
        partial, _ = lax.optimization_barrier(
            (leading_dot(forward_inverse[panel_index], adjusted), lead)
        )
        lower_list.append(reduce_col(partial, upper_partial if step == panels - 1 else None))
    lower_head = jnp.stack(lower_list)
    panel_rows = lower_head.shape[1]
    early = panels - 1
    n_row = lax.axis_size("row")
    outer = n_row // ROW_INNER
    me_core = sub_index("row", ROW_INNER, "inner")
    me_y = sub_index("row", ROW_INNER, "outer")
    other_core = shift_pairs(n_row, ROW_INNER, "inner", 1)
    piece_rows = forward_slab.shape[2] // n_row
    early_slab = forward_slab[:early].reshape(early * panel_rows, forward_slab.shape[2])
    early_lower = lower_head[:early].reshape(early * panel_rows, classes)
    early_grid = with_layout_constraint(
        leading_dot(early_slab, early_lower), Layout(major_to_minor=(0, 1))
    ).reshape(outer, ROW_INNER, piece_rows, classes)
    early_mine = lax.dynamic_index_in_dim(early_grid, me_core, 1, keepdims=False)
    early_theirs = lax.dynamic_index_in_dim(early_grid, 1 - me_core, 1, keepdims=False)
    early_got = lax.ppermute(early_theirs.astype(jnp.bfloat16), "row", other_core)
    partner_slab = lax.ppermute(forward_slab[early], "row", other_core)
    partner_lower = lax.ppermute(lower_head[early], "row", other_core)
    last = with_layout_constraint(
        leading_dot(forward_slab[early], lower_head[early])
        + leading_dot(partner_slab, partner_lower),
        Layout(major_to_minor=(0, 1)),
    ).reshape(outer, ROW_INNER, piece_rows, classes)
    pair = (
        early_mine
        + early_got.astype(jnp.float32)
        + lax.dynamic_index_in_dim(last, me_core, 1, keepdims=False)
    )
    half = pair.astype(jnp.bfloat16)
    lower_update = lax.dynamic_index_in_dim(pair, me_y, 0, keepdims=False)
    for d in range(1, outer):
        sel = lax.dynamic_index_in_dim(half, (me_y + d) % outer, 0, keepdims=False)
        lower_update = lower_update + lax.ppermute(
            sel, "row", shift_pairs(n_row, ROW_INNER, "outer", d)
        ).astype(jnp.float32)
    lower_tail = (forward_tail.astype(jnp.float32) - lower_update).astype(jnp.bfloat16)
    upper_update = lax.psum_scatter(
        upper_partial,
        "col",
        scatter_dimension=0,
        tiled=True,
    ).astype(jnp.float32)
    upper_tail = (backward_tail.astype(jnp.float32) - upper_update).astype(jnp.bfloat16)
    return (lower_head, lower_tail, upper_head, upper_tail)


def solution(mesh):
    in_specs = (
        P(None, "col", None),
        P(("col", "row"), None),
        P(None, "col", "row"),
        P(None, "row", "col"),
        P(None, "row", "col"),
        P(None, "row", None),
        P(("row", "col"), None),
        P(None, "col", "row"),
        P(None, "row", "col"),
        P("row", None, "col"),
    )
    out_specs = (
        P(None, "row", None),
        P(("col", "row"), None),
        P(None, "col", None),
        P(("row", "col"), None),
    )
    return jax.shard_map(local, mesh=mesh, in_specs=in_specs, out_specs=out_specs, check_vma=False)
```

```python
import jax
import jax.numpy as jnp
from jax import lax
from jax.experimental.layout import Layout, with_layout_constraint
from jax.sharding import PartitionSpec as P

ROW_INNER = 2
COL_INNER = 4


def shift_pairs(n, inner, sub, d):
    outer = n // inner
    pairs = []
    for o in range(outer):
        for i in range(inner):
            if sub == "inner":
                pairs.append((o * inner + i, o * inner + (i + d) % inner))
            else:
                pairs.append((o * inner + i, ((o + d) % outer) * inner + i))
    return pairs


def sub_index(axis, inner, sub):
    a = lax.axis_index(axis)
    return a % inner if sub == "inner" else a // inner


def sub_size(n, inner, sub):
    return inner if sub == "inner" else n // inner


def ar_direct(v, axis, n, inner, sub):
    size = sub_size(n, inner, sub)
    acc = v.astype(jnp.float32)
    send = v.astype(jnp.bfloat16)
    for d in range(1, size):
        acc = acc + lax.ppermute(send, axis, shift_pairs(n, inner, sub, d)).astype(jnp.float32)
    return acc


def rs_direct(v, axis, n, inner, sub):
    size = sub_size(n, inner, sub)
    me = sub_index(axis, inner, sub)
    pieces = v.reshape(size, v.shape[0] // size, v.shape[1])
    acc = lax.dynamic_index_in_dim(pieces, me, 0, keepdims=False).astype(jnp.float32)
    for d in range(1, size):
        sel = lax.dynamic_index_in_dim(pieces, (me + d) % size, 0, keepdims=False)
        acc = acc + lax.ppermute(
            sel.astype(jnp.bfloat16), axis, shift_pairs(n, inner, sub, d)
        ).astype(jnp.float32)
    return acc


def ag_direct(p, axis, n, inner, sub):
    size = sub_size(n, inner, sub)
    me = sub_index(axis, inner, sub)
    got = [p] + [lax.ppermute(p, axis, shift_pairs(n, inner, sub, -d)) for d in range(1, size)]
    stacked = jnp.roll(jnp.stack(got), me, axis=0)
    return stacked.reshape(size * p.shape[0], p.shape[1])


def rs_hier(value, axis, inner):
    n = lax.axis_size(axis)
    outer = n // inner
    rows = value.shape[0] // n
    me_in = sub_index(axis, inner, "inner")
    me_out = sub_index(axis, inner, "outer")
    grid = value.reshape(outer, inner, rows, value.shape[1])
    received = None
    for d in range(1, inner):
        sel = lax.dynamic_index_in_dim(grid, (me_in + d) % inner, 1, keepdims=False)
        got = lax.ppermute(sel, axis, shift_pairs(n, inner, "inner", d)).astype(jnp.float32)
        received = got if received is None else received + got
    acc = lax.dynamic_index_in_dim(grid, me_in, 1, keepdims=False).astype(jnp.float32) + received
    half = acc.astype(jnp.bfloat16)
    total = lax.dynamic_index_in_dim(
        lax.dynamic_index_in_dim(grid, me_in, 1, keepdims=False), me_out, 0, keepdims=False
    ).astype(jnp.float32) + lax.dynamic_index_in_dim(received, me_out, 0, keepdims=False)
    for d in range(1, outer):
        sel = lax.dynamic_index_in_dim(half, (me_out + d) % outer, 0, keepdims=False)
        total = total + lax.ppermute(sel, axis, shift_pairs(n, inner, "outer", d)).astype(jnp.float32)
    return total


def allreduce(value, axis, inner, hold=None):
    n = lax.axis_size(axis)
    piece = rs_direct(value.astype(jnp.bfloat16), axis, n, inner, "inner")
    piece = ar_direct(piece.astype(jnp.bfloat16), axis, n, inner, "outer").astype(jnp.bfloat16)
    if hold is not None:
        piece, _ = lax.optimization_barrier((piece, hold))
    return ag_direct(piece, axis, n, inner, "inner")


def reduce_row(value):
    return allreduce(value, "row", ROW_INNER)


def reduce_col(value, hold=None):
    return allreduce(value, "col", COL_INNER, hold)


def leading_dot(left, right):
    return lax.dot_general(
        left, right, (((0,), (0,)), ((), ())), preferred_element_type=jnp.float32
    )


def local(
    forward_head,
    forward_tail,
    forward_inverse,
    forward_coupling,
    forward_slab,
    backward_head,
    backward_tail,
    backward_inverse,
    backward_coupling,
    backward_slab,
):
    classes = forward_head.shape[2]
    panels = forward_head.shape[0]
    upper_list = [None] * panels
    lower_list = []
    for step in range(panels):
        panel_index = panels - 1 - step
        if panel_index == panels - 1:
            shifted = backward_head[panel_index]
        else:
            summed = None
            for later_panel in range(panel_index + 1, panels):
                block = backward_coupling[later_panel * (later_panel - 1) // 2 + panel_index]
                product = jnp.dot(
                    block, upper_list[later_panel], preferred_element_type=jnp.float32
                )
                summed = product if summed is None else summed + product
            pulled = reduce_col(summed).astype(jnp.float32)
            shifted = (backward_head[panel_index].astype(jnp.float32) - pulled).astype(jnp.bfloat16)
        upper_list[panel_index] = reduce_row(
            jnp.dot(backward_inverse[panel_index], shifted, preferred_element_type=jnp.float32)
        )

        panel_index = step
        if panel_index == 0:
            adjusted = forward_head[0]
        else:
            summed = leading_dot(
                forward_coupling[panel_index * (panel_index - 1) // 2], lower_list[0]
            )
            for earlier in range(1, panel_index):
                summed = summed + leading_dot(
                    forward_coupling[panel_index * (panel_index - 1) // 2 + earlier],
                    lower_list[earlier],
                )
            coupling = reduce_row(summed).astype(jnp.float32)
            adjusted = (forward_head[panel_index].astype(jnp.float32) - coupling).astype(
                jnp.bfloat16
            )
        lead = shifted
        if step == panels - 1:
            upper_head = jnp.stack(upper_list)
            panel_cols = upper_head.shape[1]
            flat_back = backward_slab.reshape(backward_slab.shape[0], panels * panel_cols)
            flat_upper = upper_head.reshape(panels * panel_cols, classes)
            upper_partial = with_layout_constraint(
                jnp.dot(flat_back, flat_upper, preferred_element_type=jnp.float32).astype(
                    jnp.bfloat16
                ),
                Layout(major_to_minor=(0, 1)),
            )
        partial, _ = lax.optimization_barrier(
            (leading_dot(forward_inverse[panel_index], adjusted), lead)
        )
        lower_list.append(reduce_col(partial, upper_partial if step == panels - 1 else None))
    lower_head = jnp.stack(lower_list)
    panel_rows = lower_head.shape[1]
    early = panels - 1
    early_slab = forward_slab[:early].reshape(early * panel_rows, forward_slab.shape[2])
    split = 512 if classes > 512 else classes
    updates = []
    for lo, hi in ((0, split), (split, classes)):
        if hi <= lo:
            continue
        part = lower_head[:, :, lo:hi]
        early_partial = with_layout_constraint(
            leading_dot(early_slab, part[:early].reshape(early * panel_rows, hi - lo)),
            Layout(major_to_minor=(0, 1)),
        )
        lower_partial = with_layout_constraint(
            (early_partial + leading_dot(forward_slab[early], part[early])).astype(jnp.bfloat16),
            Layout(major_to_minor=(0, 1)),
        )
        updates.append(rs_hier(lower_partial, "row", ROW_INNER))
    lower_update = jnp.concatenate(updates, axis=1)
    lower_tail = (forward_tail.astype(jnp.float32) - lower_update).astype(jnp.bfloat16)
    upper_update = lax.psum_scatter(
        upper_partial,
        "col",
        scatter_dimension=0,
        tiled=True,
    ).astype(jnp.float32)
    upper_tail = (backward_tail.astype(jnp.float32) - upper_update).astype(jnp.bfloat16)
    return (lower_head, lower_tail, upper_head, upper_tail)


def solution(mesh):
    in_specs = (
        P(None, "col", None),
        P(("col", "row"), None),
        P(None, "col", "row"),
        P(None, "row", "col"),
        P(None, "row", "col"),
        P(None, "row", None),
        P(("row", "col"), None),
        P(None, "col", "row"),
        P(None, "row", "col"),
        P("row", None, "col"),
    )
    out_specs = (
        P(None, "row", None),
        P(("col", "row"), None),
        P(None, "col", None),
        P(("row", "col"), None),
    )
    return jax.shard_map(local, mesh=mesh, in_specs=in_specs, out_specs=out_specs, check_vma=False)
```

```python
import jax
import jax.numpy as jnp
from jax import lax
from jax.experimental.layout import Layout, with_layout_constraint
from jax.sharding import PartitionSpec as P

ROW_INNER = 2
COL_INNER = 4


def shift_pairs(n, inner, sub, d):
    outer = n // inner
    pairs = []
    for o in range(outer):
        for i in range(inner):
            if sub == "inner":
                pairs.append((o * inner + i, o * inner + (i + d) % inner))
            else:
                pairs.append((o * inner + i, ((o + d) % outer) * inner + i))
    return pairs


def sub_index(axis, inner, sub):
    a = lax.axis_index(axis)
    return a % inner if sub == "inner" else a // inner


def sub_size(n, inner, sub):
    return inner if sub == "inner" else n // inner


def ar_direct(v, axis, n, inner, sub):
    size = sub_size(n, inner, sub)
    acc = v.astype(jnp.float32)
    send = v.astype(jnp.bfloat16)
    for d in range(1, size):
        acc = acc + lax.ppermute(send, axis, shift_pairs(n, inner, sub, d)).astype(jnp.float32)
    return acc


def rs_direct(v, axis, n, inner, sub):
    size = sub_size(n, inner, sub)
    me = sub_index(axis, inner, sub)
    pieces = v.reshape(size, v.shape[0] // size, v.shape[1])
    acc = lax.dynamic_index_in_dim(pieces, me, 0, keepdims=False).astype(jnp.float32)
    for d in range(1, size):
        sel = lax.dynamic_index_in_dim(pieces, (me + d) % size, 0, keepdims=False)
        acc = acc + lax.ppermute(
            sel.astype(jnp.bfloat16), axis, shift_pairs(n, inner, sub, d)
        ).astype(jnp.float32)
    return acc


def ag_direct(p, axis, n, inner, sub):
    size = sub_size(n, inner, sub)
    me = sub_index(axis, inner, sub)
    got = [p] + [lax.ppermute(p, axis, shift_pairs(n, inner, sub, -d)) for d in range(1, size)]
    stacked = jnp.roll(jnp.stack(got), me, axis=0)
    return stacked.reshape(size * p.shape[0], p.shape[1])


def rs_hier(value, axis, inner):
    n = lax.axis_size(axis)
    outer = n // inner
    rows = value.shape[0] // n
    me_in = sub_index(axis, inner, "inner")
    me_out = sub_index(axis, inner, "outer")
    grid = value.reshape(outer, inner, rows, value.shape[1])
    received = None
    for d in range(1, inner):
        sel = lax.dynamic_index_in_dim(grid, (me_in + d) % inner, 1, keepdims=False)
        got = lax.ppermute(sel, axis, shift_pairs(n, inner, "inner", d)).astype(jnp.float32)
        received = got if received is None else received + got
    acc = lax.dynamic_index_in_dim(grid, me_in, 1, keepdims=False).astype(jnp.float32) + received
    half = acc.astype(jnp.bfloat16)
    total = lax.dynamic_index_in_dim(
        lax.dynamic_index_in_dim(grid, me_in, 1, keepdims=False), me_out, 0, keepdims=False
    ).astype(jnp.float32) + lax.dynamic_index_in_dim(received, me_out, 0, keepdims=False)
    for d in range(1, outer):
        sel = lax.dynamic_index_in_dim(half, (me_out + d) % outer, 0, keepdims=False)
        total = total + lax.ppermute(sel, axis, shift_pairs(n, inner, "outer", d)).astype(jnp.float32)
    return total


def allreduce(value, axis, inner, hold=None):
    n = lax.axis_size(axis)
    piece = rs_direct(value.astype(jnp.bfloat16), axis, n, inner, "inner")
    piece = ar_direct(piece.astype(jnp.bfloat16), axis, n, inner, "outer").astype(jnp.bfloat16)
    if hold is not None:
        piece, _ = lax.optimization_barrier((piece, hold))
    return ag_direct(piece, axis, n, inner, "inner")


def reduce_row(value):
    return allreduce(value, "row", ROW_INNER)


def reduce_col(value, hold=None):
    return allreduce(value, "col", COL_INNER, hold)


def leading_dot(left, right):
    return lax.dot_general(
        left, right, (((0,), (0,)), ((), ())), preferred_element_type=jnp.float32
    )


def local(
    forward_head,
    forward_tail,
    forward_inverse,
    forward_coupling,
    forward_slab,
    backward_head,
    backward_tail,
    backward_inverse,
    backward_coupling,
    backward_slab,
):
    classes = forward_head.shape[2]
    panels = forward_head.shape[0]
    upper_list = [None] * panels
    lower_list = []
    for step in range(panels):
        panel_index = panels - 1 - step
        if panel_index == panels - 1:
            shifted = backward_head[panel_index]
        else:
            summed = None
            for later_panel in range(panel_index + 1, panels):
                block = backward_coupling[later_panel * (later_panel - 1) // 2 + panel_index]
                product = jnp.dot(
                    block, upper_list[later_panel], preferred_element_type=jnp.float32
                )
                summed = product if summed is None else summed + product
            pulled = reduce_col(summed).astype(jnp.float32)
            shifted = (backward_head[panel_index].astype(jnp.float32) - pulled).astype(jnp.bfloat16)
        upper_list[panel_index] = reduce_row(
            jnp.dot(backward_inverse[panel_index], shifted, preferred_element_type=jnp.float32)
        )

        panel_index = step
        if panel_index == 0:
            adjusted = forward_head[0]
        else:
            summed = leading_dot(
                forward_coupling[panel_index * (panel_index - 1) // 2], lower_list[0]
            )
            for earlier in range(1, panel_index):
                summed = summed + leading_dot(
                    forward_coupling[panel_index * (panel_index - 1) // 2 + earlier],
                    lower_list[earlier],
                )
            coupling = reduce_row(summed).astype(jnp.float32)
            adjusted = (forward_head[panel_index].astype(jnp.float32) - coupling).astype(
                jnp.bfloat16
            )
        lead = shifted
        if step == panels - 1:
            upper_head, _ = lax.optimization_barrier((jnp.stack(upper_list), adjusted))
            panel_cols = upper_head.shape[1]
            flat_back = backward_slab.reshape(backward_slab.shape[0], panels * panel_cols)
            flat_upper = upper_head.reshape(panels * panel_cols, classes)
            upper_partial = with_layout_constraint(
                jnp.dot(flat_back, flat_upper, preferred_element_type=jnp.float32).astype(
                    jnp.bfloat16
                ),
                Layout(major_to_minor=(0, 1)),
            )
        partial, _ = lax.optimization_barrier(
            (leading_dot(forward_inverse[panel_index], adjusted), lead)
        )
        lower_list.append(reduce_col(partial, upper_partial if step == panels - 1 else None))
    lower_head = jnp.stack(lower_list)
    panel_rows = lower_head.shape[1]
    early = panels - 1
    early_slab = forward_slab[:early].reshape(early * panel_rows, forward_slab.shape[2])
    split = 512 if classes > 512 else classes
    updates = []
    for lo, hi in ((0, split), (split, classes)):
        if hi <= lo:
            continue
        part = lower_head[:, :, lo:hi]
        early_partial = with_layout_constraint(
            leading_dot(early_slab, part[:early].reshape(early * panel_rows, hi - lo)),
            Layout(major_to_minor=(0, 1)),
        )
        lower_partial = with_layout_constraint(
            (early_partial + leading_dot(forward_slab[early], part[early])).astype(jnp.bfloat16),
            Layout(major_to_minor=(0, 1)),
        )
        updates.append(rs_hier(lower_partial, "row", ROW_INNER))
    lower_update = jnp.concatenate(updates, axis=1)
    lower_tail = (forward_tail.astype(jnp.float32) - lower_update).astype(jnp.bfloat16)
    upper_update = lax.psum_scatter(
        upper_partial,
        "col",
        scatter_dimension=0,
        tiled=True,
    ).astype(jnp.float32)
    upper_tail = (backward_tail.astype(jnp.float32) - upper_update).astype(jnp.bfloat16)
    return (lower_head, lower_tail, upper_head, upper_tail)


def solution(mesh):
    in_specs = (
        P(None, "col", None),
        P(("col", "row"), None),
        P(None, "col", "row"),
        P(None, "row", "col"),
        P(None, "row", "col"),
        P(None, "row", None),
        P(("row", "col"), None),
        P(None, "col", "row"),
        P(None, "row", "col"),
        P("row", None, "col"),
    )
    out_specs = (
        P(None, "row", None),
        P(("col", "row"), None),
        P(None, "col", None),
        P(("row", "col"), None),
    )
    return jax.shard_map(local, mesh=mesh, in_specs=in_specs, out_specs=out_specs, check_vma=False)
```

```python
import jax
import jax.numpy as jnp
from jax import lax
from jax.experimental.layout import Layout, with_layout_constraint
from jax.sharding import PartitionSpec as P

ROW_INNER = 2
COL_INNER = 4


def shift_pairs(n, inner, sub, d):
    outer = n // inner
    pairs = []
    for o in range(outer):
        for i in range(inner):
            if sub == "inner":
                pairs.append((o * inner + i, o * inner + (i + d) % inner))
            else:
                pairs.append((o * inner + i, ((o + d) % outer) * inner + i))
    return pairs


def sub_index(axis, inner, sub):
    a = lax.axis_index(axis)
    return a % inner if sub == "inner" else a // inner


def sub_size(n, inner, sub):
    return inner if sub == "inner" else n // inner


def ar_direct(v, axis, n, inner, sub):
    size = sub_size(n, inner, sub)
    acc = v.astype(jnp.float32)
    send = v.astype(jnp.bfloat16)
    for d in range(1, size):
        acc = acc + lax.ppermute(send, axis, shift_pairs(n, inner, sub, d)).astype(jnp.float32)
    return acc


def rs_direct(v, axis, n, inner, sub):
    size = sub_size(n, inner, sub)
    me = sub_index(axis, inner, sub)
    pieces = v.reshape(size, v.shape[0] // size, v.shape[1])
    acc = lax.dynamic_index_in_dim(pieces, me, 0, keepdims=False).astype(jnp.float32)
    for d in range(1, size):
        sel = lax.dynamic_index_in_dim(pieces, (me + d) % size, 0, keepdims=False)
        acc = acc + lax.ppermute(
            sel.astype(jnp.bfloat16), axis, shift_pairs(n, inner, sub, d)
        ).astype(jnp.float32)
    return acc


def ag_direct(p, axis, n, inner, sub):
    size = sub_size(n, inner, sub)
    me = sub_index(axis, inner, sub)
    got = [p] + [lax.ppermute(p, axis, shift_pairs(n, inner, sub, -d)) for d in range(1, size)]
    stacked = jnp.roll(jnp.stack(got), me, axis=0)
    return stacked.reshape(size * p.shape[0], p.shape[1])


def rs_hier(value, axis, inner):
    n = lax.axis_size(axis)
    outer = n // inner
    rows = value.shape[0] // n
    me_in = sub_index(axis, inner, "inner")
    me_out = sub_index(axis, inner, "outer")
    grid = value.reshape(outer, inner, rows, value.shape[1])
    received = None
    for d in range(1, inner):
        sel = lax.dynamic_index_in_dim(grid, (me_in + d) % inner, 1, keepdims=False)
        got = lax.ppermute(sel, axis, shift_pairs(n, inner, "inner", d)).astype(jnp.float32)
        received = got if received is None else received + got
    acc = lax.dynamic_index_in_dim(grid, me_in, 1, keepdims=False).astype(jnp.float32) + received
    half = acc.astype(jnp.bfloat16)
    total = lax.dynamic_index_in_dim(
        lax.dynamic_index_in_dim(grid, me_in, 1, keepdims=False), me_out, 0, keepdims=False
    ).astype(jnp.float32) + lax.dynamic_index_in_dim(received, me_out, 0, keepdims=False)
    for d in range(1, outer):
        sel = lax.dynamic_index_in_dim(half, (me_out + d) % outer, 0, keepdims=False)
        total = total + lax.ppermute(sel, axis, shift_pairs(n, inner, "outer", d)).astype(jnp.float32)
    return total


def allreduce(value, axis, inner, hold=None):
    n = lax.axis_size(axis)
    piece = rs_direct(value.astype(jnp.bfloat16), axis, n, inner, "inner")
    piece = ar_direct(piece.astype(jnp.bfloat16), axis, n, inner, "outer").astype(jnp.bfloat16)
    if hold is not None:
        piece, _ = lax.optimization_barrier((piece, hold))
    return ag_direct(piece, axis, n, inner, "inner")


def reduce_row(value):
    return allreduce(value, "row", ROW_INNER)


def reduce_col(value, hold=None):
    return allreduce(value, "col", COL_INNER, hold)


def leading_dot(left, right):
    return lax.dot_general(
        left, right, (((0,), (0,)), ((), ())), preferred_element_type=jnp.float32
    )


def local(
    forward_head,
    forward_tail,
    forward_inverse,
    forward_coupling,
    forward_slab,
    backward_head,
    backward_tail,
    backward_inverse,
    backward_coupling,
    backward_slab,
):
    classes = forward_head.shape[2]
    panels = forward_head.shape[0]
    upper_list = [None] * panels
    lower_list = []
    for step in range(panels):
        panel_index = panels - 1 - step
        if panel_index == panels - 1:
            shifted = backward_head[panel_index]
            backward_lead = shifted
        else:
            summed = None
            for later_panel in range(panel_index + 1, panels):
                block = backward_coupling[later_panel * (later_panel - 1) // 2 + panel_index]
                product = jnp.dot(
                    block, upper_list[later_panel], preferred_element_type=jnp.float32
                )
                summed = product if summed is None else summed + product
            backward_lead = summed
            pulled = reduce_col(summed).astype(jnp.float32)
            shifted = (backward_head[panel_index].astype(jnp.float32) - pulled).astype(jnp.bfloat16)
        upper_list[panel_index] = reduce_row(
            jnp.dot(backward_inverse[panel_index], shifted, preferred_element_type=jnp.float32)
        )

        panel_index = step
        if panel_index == 0:
            adjusted = forward_head[0]
        else:
            summed = leading_dot(
                forward_coupling[panel_index * (panel_index - 1) // 2], lower_list[0]
            )
            for earlier in range(1, panel_index):
                summed = summed + leading_dot(
                    forward_coupling[panel_index * (panel_index - 1) // 2 + earlier],
                    lower_list[earlier],
                )
            coupling = reduce_row(summed).astype(jnp.float32)
            adjusted = (forward_head[panel_index].astype(jnp.float32) - coupling).astype(
                jnp.bfloat16
            )
        lead = backward_lead
        if step == panels - 1:
            upper_head = jnp.stack(upper_list)
            panel_cols = upper_head.shape[1]
            flat_back = backward_slab.reshape(backward_slab.shape[0], panels * panel_cols)
            flat_upper = upper_head.reshape(panels * panel_cols, classes)
            upper_partial = with_layout_constraint(
                jnp.dot(flat_back, flat_upper, preferred_element_type=jnp.float32).astype(
                    jnp.bfloat16
                ),
                Layout(major_to_minor=(0, 1)),
            )
        partial, _ = lax.optimization_barrier(
            (leading_dot(forward_inverse[panel_index], adjusted), lead)
        )
        lower_list.append(reduce_col(partial, upper_partial if step == panels - 1 else None))
    lower_head = jnp.stack(lower_list)
    panel_rows = lower_head.shape[1]
    early = panels - 1
    early_slab = forward_slab[:early].reshape(early * panel_rows, forward_slab.shape[2])
    split = 512 if classes > 512 else classes
    updates = []
    for lo, hi in ((0, split), (split, classes)):
        if hi <= lo:
            continue
        part = lower_head[:, :, lo:hi]
        early_partial = with_layout_constraint(
            leading_dot(early_slab, part[:early].reshape(early * panel_rows, hi - lo)),
            Layout(major_to_minor=(0, 1)),
        )
        lower_partial = with_layout_constraint(
            (early_partial + leading_dot(forward_slab[early], part[early])).astype(jnp.bfloat16),
            Layout(major_to_minor=(0, 1)),
        )
        updates.append(rs_hier(lower_partial, "row", ROW_INNER))
    lower_update = jnp.concatenate(updates, axis=1)
    lower_tail = (forward_tail.astype(jnp.float32) - lower_update).astype(jnp.bfloat16)
    upper_update = lax.psum_scatter(
        upper_partial,
        "col",
        scatter_dimension=0,
        tiled=True,
    ).astype(jnp.float32)
    upper_tail = (backward_tail.astype(jnp.float32) - upper_update).astype(jnp.bfloat16)
    return (lower_head, lower_tail, upper_head, upper_tail)


def solution(mesh):
    in_specs = (
        P(None, "col", None),
        P(("col", "row"), None),
        P(None, "col", "row"),
        P(None, "row", "col"),
        P(None, "row", "col"),
        P(None, "row", None),
        P(("row", "col"), None),
        P(None, "col", "row"),
        P(None, "row", "col"),
        P("row", None, "col"),
    )
    out_specs = (
        P(None, "row", None),
        P(("col", "row"), None),
        P(None, "col", None),
        P(("row", "col"), None),
    )
    return jax.shard_map(local, mesh=mesh, in_specs=in_specs, out_specs=out_specs, check_vma=False)
```

```python
import jax
import jax.numpy as jnp
from jax import lax
from jax.experimental.layout import Layout, with_layout_constraint
from jax.sharding import PartitionSpec as P

ROW_INNER = 2
COL_INNER = 4


def shift_pairs(n, inner, sub, d):
    outer = n // inner
    pairs = []
    for o in range(outer):
        for i in range(inner):
            if sub == "inner":
                pairs.append((o * inner + i, o * inner + (i + d) % inner))
            else:
                pairs.append((o * inner + i, ((o + d) % outer) * inner + i))
    return pairs


def sub_index(axis, inner, sub):
    a = lax.axis_index(axis)
    return a % inner if sub == "inner" else a // inner


def sub_size(n, inner, sub):
    return inner if sub == "inner" else n // inner


def ar_direct(v, axis, n, inner, sub):
    size = sub_size(n, inner, sub)
    acc = v.astype(jnp.float32)
    send = v.astype(jnp.bfloat16)
    for d in range(1, size):
        acc = acc + lax.ppermute(send, axis, shift_pairs(n, inner, sub, d)).astype(jnp.float32)
    return acc


def rs_direct(v, axis, n, inner, sub):
    size = sub_size(n, inner, sub)
    me = sub_index(axis, inner, sub)
    pieces = v.reshape(size, v.shape[0] // size, v.shape[1])
    acc = lax.dynamic_index_in_dim(pieces, me, 0, keepdims=False).astype(jnp.float32)
    for d in range(1, size):
        sel = lax.dynamic_index_in_dim(pieces, (me + d) % size, 0, keepdims=False)
        acc = acc + lax.ppermute(
            sel.astype(jnp.bfloat16), axis, shift_pairs(n, inner, sub, d)
        ).astype(jnp.float32)
    return acc


def ag_direct(p, axis, n, inner, sub):
    size = sub_size(n, inner, sub)
    me = sub_index(axis, inner, sub)
    got = [p] + [lax.ppermute(p, axis, shift_pairs(n, inner, sub, -d)) for d in range(1, size)]
    stacked = jnp.roll(jnp.stack(got), me, axis=0)
    return stacked.reshape(size * p.shape[0], p.shape[1])


def rs_hier(value, axis, inner):
    n = lax.axis_size(axis)
    outer = n // inner
    rows = value.shape[0] // n
    me_in = sub_index(axis, inner, "inner")
    me_out = sub_index(axis, inner, "outer")
    grid = value.reshape(outer, inner, rows, value.shape[1])
    received = None
    for d in range(1, inner):
        sel = lax.dynamic_index_in_dim(grid, (me_in + d) % inner, 1, keepdims=False)
        got = lax.ppermute(sel, axis, shift_pairs(n, inner, "inner", d)).astype(jnp.float32)
        received = got if received is None else received + got
    acc = lax.dynamic_index_in_dim(grid, me_in, 1, keepdims=False).astype(jnp.float32) + received
    half = acc.astype(jnp.bfloat16)
    total = lax.dynamic_index_in_dim(
        lax.dynamic_index_in_dim(grid, me_in, 1, keepdims=False), me_out, 0, keepdims=False
    ).astype(jnp.float32) + lax.dynamic_index_in_dim(received, me_out, 0, keepdims=False)
    for d in range(1, outer):
        sel = lax.dynamic_index_in_dim(half, (me_out + d) % outer, 0, keepdims=False)
        total = total + lax.ppermute(sel, axis, shift_pairs(n, inner, "outer", d)).astype(jnp.float32)
    return total


def allreduce(value, axis, inner, hold=None):
    n = lax.axis_size(axis)
    piece = rs_direct(value.astype(jnp.bfloat16), axis, n, inner, "inner")
    piece = ar_direct(piece.astype(jnp.bfloat16), axis, n, inner, "outer").astype(jnp.bfloat16)
    if hold is not None:
        piece, _ = lax.optimization_barrier((piece, hold))
    return ag_direct(piece, axis, n, inner, "inner")


def reduce_row(value):
    return allreduce(value, "row", ROW_INNER)


def reduce_col(value, hold=None):
    return allreduce(value, "col", COL_INNER, hold)


def leading_dot(left, right):
    return lax.dot_general(
        left, right, (((0,), (0,)), ((), ())), preferred_element_type=jnp.float32
    )


def local(
    forward_head,
    forward_tail,
    forward_inverse,
    forward_coupling,
    forward_slab,
    backward_head,
    backward_tail,
    backward_inverse,
    backward_coupling,
    backward_slab,
):
    classes = forward_head.shape[2]
    panels = forward_head.shape[0]
    upper_list = [None] * panels
    lower_list = []
    for step in range(panels):
        panel_index = panels - 1 - step
        if panel_index == panels - 1:
            shifted = backward_head[panel_index]
        else:
            summed = None
            for later_panel in range(panel_index + 1, panels):
                block = backward_coupling[later_panel * (later_panel - 1) // 2 + panel_index]
                product = jnp.dot(
                    block, upper_list[later_panel], preferred_element_type=jnp.float32
                )
                summed = product if summed is None else summed + product
            pulled = reduce_col(summed).astype(jnp.float32)
            shifted = (backward_head[panel_index].astype(jnp.float32) - pulled).astype(jnp.bfloat16)
        upper_list[panel_index] = reduce_row(
            jnp.dot(backward_inverse[panel_index], shifted, preferred_element_type=jnp.float32)
        )

        panel_index = step
        if panel_index == 0:
            adjusted = forward_head[0]
        else:
            summed = leading_dot(
                forward_coupling[panel_index * (panel_index - 1) // 2], lower_list[0]
            )
            for earlier in range(1, panel_index):
                summed = summed + leading_dot(
                    forward_coupling[panel_index * (panel_index - 1) // 2 + earlier],
                    lower_list[earlier],
                )
            coupling = reduce_row(summed).astype(jnp.float32)
            adjusted = (forward_head[panel_index].astype(jnp.float32) - coupling).astype(
                jnp.bfloat16
            )
        lead = shifted
        if step == panels - 1:
            upper_head = jnp.stack(upper_list)
            panel_cols = upper_head.shape[1]
            flat_back = backward_slab.reshape(backward_slab.shape[0], panels * panel_cols)
            flat_upper = upper_head.reshape(panels * panel_cols, classes)
            upper_partial = with_layout_constraint(
                jnp.dot(flat_back, flat_upper, preferred_element_type=jnp.float32).astype(
                    jnp.bfloat16
                ),
                Layout(major_to_minor=(0, 1)),
            )
        partial, _ = lax.optimization_barrier(
            (leading_dot(forward_inverse[panel_index], adjusted), lead)
        )
        lower_list.append(reduce_col(partial, upper_partial if step == panels - 1 else None))
    lower_head = jnp.stack(lower_list)
    panel_rows = lower_head.shape[1]
    early = panels - 1
    early_slab = forward_slab[:early].reshape(early * panel_rows, forward_slab.shape[2])
    split = 512 if classes > 512 else classes
    updates = []
    for lo, hi in ((0, split), (split, classes)):
        if hi <= lo:
            continue
        part = lower_head[:, :, lo:hi]
        early_partial = with_layout_constraint(
            leading_dot(early_slab, part[:early].reshape(early * panel_rows, hi - lo)).astype(
                jnp.bfloat16
            ),
            Layout(major_to_minor=(0, 1)),
        ).astype(jnp.float32)
        lower_partial = with_layout_constraint(
            (early_partial + leading_dot(forward_slab[early], part[early])).astype(jnp.bfloat16),
            Layout(major_to_minor=(0, 1)),
        )
        updates.append(rs_hier(lower_partial, "row", ROW_INNER))
    lower_update = jnp.concatenate(updates, axis=1)
    lower_tail = (forward_tail.astype(jnp.float32) - lower_update).astype(jnp.bfloat16)
    upper_update = lax.psum_scatter(
        upper_partial,
        "col",
        scatter_dimension=0,
        tiled=True,
    ).astype(jnp.float32)
    upper_tail = (backward_tail.astype(jnp.float32) - upper_update).astype(jnp.bfloat16)
    return (lower_head, lower_tail, upper_head, upper_tail)


def solution(mesh):
    in_specs = (
        P(None, "col", None),
        P(("col", "row"), None),
        P(None, "col", "row"),
        P(None, "row", "col"),
        P(None, "row", "col"),
        P(None, "row", None),
        P(("row", "col"), None),
        P(None, "col", "row"),
        P(None, "row", "col"),
        P("row", None, "col"),
    )
    out_specs = (
        P(None, "row", None),
        P(("col", "row"), None),
        P(None, "col", None),
        P(("row", "col"), None),
    )
    return jax.shard_map(local, mesh=mesh, in_specs=in_specs, out_specs=out_specs, check_vma=False)
```

```python
import jax
import jax.numpy as jnp
from jax import lax
from jax.experimental.layout import Layout, with_layout_constraint
from jax.sharding import PartitionSpec as P

ROW_INNER = 2
COL_INNER = 4


def shift_pairs(n, inner, sub, d):
    outer = n // inner
    pairs = []
    for o in range(outer):
        for i in range(inner):
            if sub == "inner":
                pairs.append((o * inner + i, o * inner + (i + d) % inner))
            else:
                pairs.append((o * inner + i, ((o + d) % outer) * inner + i))
    return pairs


def sub_index(axis, inner, sub):
    a = lax.axis_index(axis)
    return a % inner if sub == "inner" else a // inner


def sub_size(n, inner, sub):
    return inner if sub == "inner" else n // inner


def ar_direct(v, axis, n, inner, sub):
    size = sub_size(n, inner, sub)
    acc = v.astype(jnp.float32)
    send = v.astype(jnp.bfloat16)
    for d in range(1, size):
        acc = acc + lax.ppermute(send, axis, shift_pairs(n, inner, sub, d)).astype(jnp.float32)
    return acc


def rs_direct(v, axis, n, inner, sub):
    size = sub_size(n, inner, sub)
    me = sub_index(axis, inner, sub)
    pieces = v.reshape(size, v.shape[0] // size, v.shape[1])
    acc = lax.dynamic_index_in_dim(pieces, me, 0, keepdims=False).astype(jnp.float32)
    for d in range(1, size):
        sel = lax.dynamic_index_in_dim(pieces, (me + d) % size, 0, keepdims=False)
        acc = acc + lax.ppermute(
            sel.astype(jnp.bfloat16), axis, shift_pairs(n, inner, sub, d)
        ).astype(jnp.float32)
    return acc


def ag_direct(p, axis, n, inner, sub):
    size = sub_size(n, inner, sub)
    me = sub_index(axis, inner, sub)
    got = [p] + [lax.ppermute(p, axis, shift_pairs(n, inner, sub, -d)) for d in range(1, size)]
    stacked = jnp.roll(jnp.stack(got), me, axis=0)
    return stacked.reshape(size * p.shape[0], p.shape[1])


def rs_hier(value, axis, inner):
    n = lax.axis_size(axis)
    outer = n // inner
    rows = value.shape[0] // n
    me_in = sub_index(axis, inner, "inner")
    me_out = sub_index(axis, inner, "outer")
    grid = value.reshape(outer, inner, rows, value.shape[1])
    received = None
    for d in range(1, inner):
        sel = lax.dynamic_index_in_dim(grid, (me_in + d) % inner, 1, keepdims=False)
        got = lax.ppermute(sel, axis, shift_pairs(n, inner, "inner", d)).astype(jnp.float32)
        received = got if received is None else received + got
    acc = lax.dynamic_index_in_dim(grid, me_in, 1, keepdims=False).astype(jnp.float32) + received
    half = acc.astype(jnp.bfloat16)
    total = lax.dynamic_index_in_dim(
        lax.dynamic_index_in_dim(grid, me_in, 1, keepdims=False), me_out, 0, keepdims=False
    ).astype(jnp.float32) + lax.dynamic_index_in_dim(received, me_out, 0, keepdims=False)
    for d in range(1, outer):
        sel = lax.dynamic_index_in_dim(half, (me_out + d) % outer, 0, keepdims=False)
        total = total + lax.ppermute(sel, axis, shift_pairs(n, inner, "outer", d)).astype(jnp.float32)
    return total


def allreduce(value, axis, inner, hold=None):
    n = lax.axis_size(axis)
    piece = rs_direct(value.astype(jnp.bfloat16), axis, n, inner, "inner")
    piece = ar_direct(piece.astype(jnp.bfloat16), axis, n, inner, "outer").astype(jnp.bfloat16)
    if hold is not None:
        piece, _ = lax.optimization_barrier((piece, hold))
    return ag_direct(piece, axis, n, inner, "inner")


def reduce_row(value):
    return allreduce(value, "row", ROW_INNER)


def reduce_col(value, hold=None):
    return allreduce(value, "col", COL_INNER, hold)


def leading_dot(left, right):
    return lax.dot_general(
        left, right, (((0,), (0,)), ((), ())), preferred_element_type=jnp.float32
    )


def local(
    forward_head,
    forward_tail,
    forward_inverse,
    forward_coupling,
    forward_slab,
    backward_head,
    backward_tail,
    backward_inverse,
    backward_coupling,
    backward_slab,
):
    classes = forward_head.shape[2]
    panels = forward_head.shape[0]
    upper_list = [None] * panels
    lower_list = []
    for step in range(panels):
        panel_index = panels - 1 - step
        if panel_index == panels - 1:
            shifted = backward_head[panel_index]
        else:
            summed = None
            for later_panel in range(panel_index + 1, panels):
                block = backward_coupling[later_panel * (later_panel - 1) // 2 + panel_index]
                product = jnp.dot(
                    block, upper_list[later_panel], preferred_element_type=jnp.float32
                )
                summed = product if summed is None else summed + product
            pulled = reduce_col(summed).astype(jnp.float32)
            shifted = (backward_head[panel_index].astype(jnp.float32) - pulled).astype(jnp.bfloat16)
        upper_list[panel_index] = reduce_row(
            jnp.dot(backward_inverse[panel_index], shifted, preferred_element_type=jnp.float32)
        )

        panel_index = step
        if panel_index == 0:
            adjusted = forward_head[0]
        else:
            summed = leading_dot(
                forward_coupling[panel_index * (panel_index - 1) // 2], lower_list[0]
            )
            for earlier in range(1, panel_index):
                summed = summed + leading_dot(
                    forward_coupling[panel_index * (panel_index - 1) // 2 + earlier],
                    lower_list[earlier],
                )
            coupling = reduce_row(summed).astype(jnp.float32)
            adjusted = (forward_head[panel_index].astype(jnp.float32) - coupling).astype(
                jnp.bfloat16
            )
        lead = shifted
        if step == panels - 1:
            upper_head = jnp.stack(upper_list)
            panel_cols = upper_head.shape[1]
            flat_back = backward_slab.reshape(backward_slab.shape[0], panels * panel_cols)
            flat_upper = upper_head.reshape(panels * panel_cols, classes)
            upper_partial = with_layout_constraint(
                jnp.dot(flat_back, flat_upper, preferred_element_type=jnp.float32).astype(
                    jnp.bfloat16
                ),
                Layout(major_to_minor=(0, 1)),
            )
        partial, _ = lax.optimization_barrier(
            (leading_dot(forward_inverse[panel_index], adjusted), lead)
        )
        lower_list.append(reduce_col(partial, upper_partial if step == panels - 1 else None))
    lower_head = jnp.stack(lower_list)
    panel_rows = lower_head.shape[1]
    early = panels - 1
    early_slab = forward_slab[:early].reshape(early * panel_rows, forward_slab.shape[2])
    split = classes
    updates = []
    for lo, hi in ((0, split), (split, classes)):
        if hi <= lo:
            continue
        part = lower_head[:, :, lo:hi]
        early_partial = with_layout_constraint(
            leading_dot(early_slab, part[:early].reshape(early * panel_rows, hi - lo)).astype(
                jnp.bfloat16
            ),
            Layout(major_to_minor=(0, 1)),
        ).astype(jnp.float32)
        lower_partial = with_layout_constraint(
            (early_partial + leading_dot(forward_slab[early], part[early])).astype(jnp.bfloat16),
            Layout(major_to_minor=(0, 1)),
        )
        updates.append(rs_hier(lower_partial, "row", ROW_INNER))
    lower_update = jnp.concatenate(updates, axis=1)
    lower_tail = (forward_tail.astype(jnp.float32) - lower_update).astype(jnp.bfloat16)
    upper_update = lax.psum_scatter(
        upper_partial,
        "col",
        scatter_dimension=0,
        tiled=True,
    ).astype(jnp.float32)
    upper_tail = (backward_tail.astype(jnp.float32) - upper_update).astype(jnp.bfloat16)
    return (lower_head, lower_tail, upper_head, upper_tail)


def solution(mesh):
    in_specs = (
        P(None, "col", None),
        P(("col", "row"), None),
        P(None, "col", "row"),
        P(None, "row", "col"),
        P(None, "row", "col"),
        P(None, "row", None),
        P(("row", "col"), None),
        P(None, "col", "row"),
        P(None, "row", "col"),
        P("row", None, "col"),
    )
    out_specs = (
        P(None, "row", None),
        P(("col", "row"), None),
        P(None, "col", None),
        P(("row", "col"), None),
    )
    return jax.shard_map(local, mesh=mesh, in_specs=in_specs, out_specs=out_specs, check_vma=False)
```
